32 devices in a mesh: band: 2 (over x), spk: 16 (over z, y, core).
Axes of the slice: x: 2, y: 2, z: 4, core: 2. Of those that a mesh axis runs over, the one named last changes fastest.
Arguments:
- direction: float32 [64, 128, 128], P(('band', 'spk')), parts along dimension 0, may hold values from -6 to 6
- plant: bfloat16 [832, 2, 128, 128], P(('band', 'spk')), parts along dimension 0
- tile_pairs: int32 [832, 2], P(('band', 'spk')), parts along dimension 0, may hold values from 0 to 127, as said below
- mic_weight: float32 [2, 128, 128], P('band', 'spk'), parts along dimension 0, may hold values from 0.3 to 3
Outputs:
- hessian_vector: float32 [64, 128, 128], P(('band', 'spk')), parts along dimension 0
The draws below stay inside these ranges and needn't reach their ends.
There are 2 independent parts, one for each index of `band`. The reference program is written for one: setup_inputs(seed, part) draws one part's arguments, and reference() takes and returns one part's arrays. A program takes and returns all parts, laid end to end along the dimension named above; each array names one. Nothing has to cross between parts.
Inputs may be any that keep to these rules, and one draw needn't show every extreme that they name: `tile_pairs`: column 0 is a speaker block, column 1 a microphone block. The rows of one device (aligned blocks of 26 rows) all lie in that device's bin, and their speaker blocks s satisfy s // 2 = (device index) % 16; no pair repeats on a device. Counting microphone blocks m by the device m * 16 // 128, at most 4 rows of one device fall to any one device, and in every part one device gets exactly 4 from every device.
All inputs are finite; a program needn't handle non-finite values.
Results may differ from the reference program's by a relative error of at most 0.0032.
Values may be sent and summed in bfloat16 or wider, within the bound.
No kernel may reach another device: no remote copies, remote signals or barrier semaphores. Data moves between devices by JAX's collectives and lax.ppermute only.
A program may use at most 128 MiB of HBM per device.

```python
import math
import jax
import jax.numpy as jnp
from jax import lax

BLK = 128
SBLK = 32
MBLK = 128
R = 64
UNIT_DEV = 2
SPEAKERS = 4096
BINS = 1
UNITS = 32
TILE_DEV = 26
TILES = 416
MOST = 4


def draw_plant(key, part):
    keys = jax.random.split(jax.random.fold_in(key, 11), 4)
    shape = (TILES, 2, BLK, BLK)
    base = jax.random.normal(keys[0], shape, jnp.float32)
    row_scale = jnp.power(10.0, jax.random.uniform(keys[1], (TILES, 1, BLK, 1), jnp.float32) - 0.5)
    col_scale = jnp.power(10.0, jax.random.uniform(keys[2], (TILES, 1, 1, BLK), jnp.float32) - 0.5)
    tile_scale = jnp.power(10.0, jax.random.uniform(keys[3], (TILES, 1, 1, 1), jnp.float32) - 0.5)
    values = base * row_scale * col_scale * tile_scale * (0.1 / BLK ** 0.5)
    return values.astype(jnp.bfloat16)


def draw_tile_pairs(key, part):
    devices = TILES // TILE_DEV
    slot_count = devices * MOST
    peer_blocks = MBLK // devices
    combos = UNIT_DEV * peer_blocks
    groups = SBLK // UNIT_DEV
    full_peer = jax.random.randint(jax.random.fold_in(key, 7), (), 0, devices)

    def one_device(device):
        dev_key = jax.random.fold_in(key, device + 100)
        first_key, second_key, third_key = jax.random.split(dev_key, 3)
        ranking = jax.random.permutation(first_key, slot_count)
        slot_peer = jnp.arange(slot_count) // MOST
        scores = jnp.where(slot_peer == full_peer, ranking - slot_count, ranking)
        chosen = jnp.argsort(scores, stable=True)[:TILE_DEV]
        chosen = chosen[jax.random.permutation(second_key, TILE_DEV)]

        def peer_combos(peer_key):
            return jax.random.permutation(peer_key, combos)[:MOST]
        combo_table = jax.vmap(peer_combos)(jax.random.split(third_key, devices))
        chosen_peer = chosen // MOST
        chosen_slot = chosen % MOST
        combo = combo_table[chosen_peer, chosen_slot]
        unit_local = combo // peer_blocks
        mic_block = chosen_peer * peer_blocks + combo % peer_blocks
        speaker_block = device % groups * UNIT_DEV + unit_local
        return jnp.stack([speaker_block, mic_block], axis=1)
    result = jax.vmap(one_device)(jnp.arange(devices))
    return result.reshape(TILES, 2).astype(jnp.int32)


def level_of(key, dims, pieces, least, largest):
    factor_of, own = 1.0, jax.random.fold_in(key, 6)
    for position, parts in pieces:
        heights = jnp.exp(jax.random.uniform(jax.random.fold_in(own, position), (parts,), jnp.float32, least / len(pieces), largest / len(pieces)))
        factor_of = factor_of * jnp.repeat(heights, dims[position] // parts).reshape([-1 if axis == position else 1 for axis in range(len(dims))])
    return factor_of


def scatter_about(stream_key, extent, width, bound, cuts=(), kind=jnp.bfloat16):
    loudness = level_of(stream_key, extent, cuts, -0.22, 0.18) if cuts else 1.0
    drawn = jax.random.normal(stream_key, extent, jnp.float32) * width * loudness
    return jnp.minimum(jnp.maximum(drawn, -bound), bound).astype(kind)


def setup_inputs(seed: int = 0, part: int = 0) -> dict:
    streams_of = jax.random.split(jax.random.key(seed), 5)
    own_keys = jax.random.split(jax.random.fold_in(streams_of[4], part), 5)
    return {
        "direction": scatter_about(own_keys[0], (UNITS, BLK, 2 * R), 1.0, 6.0, ((0, 16),), jnp.float32),
        "plant": draw_plant(jax.random.fold_in(jax.random.fold_in(streams_of[4], part), 71), part),
        "tile_pairs": draw_tile_pairs(jax.random.fold_in(jax.random.fold_in(streams_of[4], part), 71), part),
        "mic_weight": jnp.clip(jnp.exp(math.log(3.0) - 2.3025851 * jax.random.uniform(own_keys[3], (BINS, MBLK, BLK), jnp.float32) ** level_of(own_keys[3], (BINS, MBLK, BLK), ((1, 16),), -0.2, 0.2)), 0.3, 3.0),
    }


reg_weight = 0.25


def reference(direction, plant, tile_pairs, mic_weight):
    highest = lax.Precision.HIGHEST
    tile_index = jnp.arange(TILES, dtype=jnp.int32)
    tile_bin = ((tile_index // TILE_DEV) * UNIT_DEV // SBLK).astype(jnp.int32)
    speaker_unit = (tile_bin * SBLK + tile_pairs[:, 0]).astype(jnp.int32)
    mic_unit = (tile_bin * MBLK + tile_pairs[:, 1]).astype(jnp.int32)
    rounded = lax.optimization_barrier(direction.astype(jnp.bfloat16)).astype(jnp.float32)
    plant_wide = plant.astype(jnp.float32)
    forward = jnp.einsum('tcij,tjk->tcik', plant_wide, rounded[speaker_unit], precision=highest)
    partial_field = jnp.concatenate([forward[:, 0, :, :R] - forward[:, 1, :, R:], forward[:, 0, :, R:] + forward[:, 1, :, :R]], axis=-1)
    pressure = jax.ops.segment_sum(partial_field, mic_unit, num_segments=BINS * MBLK)
    weights_flat = mic_weight.reshape(BINS * MBLK, BLK)
    weighted = lax.optimization_barrier((weights_flat[:, :, None] * pressure).astype(jnp.bfloat16)).astype(jnp.float32)
    adjoint = jnp.einsum('tcij,tik->tcjk', plant_wide, weighted[mic_unit], precision=highest)
    back_field = jnp.concatenate([adjoint[:, 0, :, :R] + adjoint[:, 1, :, R:], adjoint[:, 0, :, R:] - adjoint[:, 1, :, :R]], axis=-1)
    gram = jax.ops.segment_sum(back_field, speaker_unit, num_segments=UNITS)
    tile_power = jnp.sum(jnp.square(plant_wide), axis=(1, 2, 3))
    bin_power = jax.ops.segment_sum(tile_power, tile_bin, num_segments=BINS)
    unit_power = jnp.repeat(bin_power, SBLK)
    return gram + reg_weight * unit_power[:, None, None] / SPEAKERS * direction
```

```python
import jax
import jax.numpy as jnp
from jax import lax
from jax.sharding import PartitionSpec as P

SBLK = 32
MBLK = 128
SPEAKERS = 4096


reg_weight = 0.25


def complex_forward(plant, field_rows):
    halfway = field_rows.shape[-1] // 2
    product = jnp.einsum("tcij,tjk->tcik", plant, field_rows, preferred_element_type=jnp.float32)
    real_part = product[:, 0, :, :halfway] - product[:, 1, :, halfway:]
    imag_part = product[:, 0, :, halfway:] + product[:, 1, :, :halfway]
    return jnp.concatenate([real_part, imag_part], axis=-1)


def complex_adjoint(plant, field_rows):
    halfway = field_rows.shape[-1] // 2
    product = jnp.einsum("tcij,tik->tcjk", plant, field_rows, preferred_element_type=jnp.float32)
    real_part = product[:, 0, :, :halfway] + product[:, 1, :, halfway:]
    imag_part = product[:, 0, :, halfway:] - product[:, 1, :, :halfway]
    return jnp.concatenate([real_part, imag_part], axis=-1)


def slot_ranks(target_peer, devices):
    onehot = (target_peer[..., :, None] == jnp.arange(devices)).astype(jnp.int32)
    running = jnp.cumsum(onehot, axis=-2)
    return jnp.take_along_axis(running, target_peer[..., None], axis=-1)[..., 0] - 1


def select(onehot, blocks):
    return jnp.einsum("st,tjk->sjk", onehot.astype(blocks.dtype), blocks,
                      preferred_element_type=jnp.float32)


def per_device(direction, plant, tile_pairs, mic_weight):
    devices = lax.axis_size("spk")
    device_id = lax.axis_index("spk")
    unit_count = direction.shape[0]
    tile_count = plant.shape[0]
    block_size = direction.shape[1]
    groups_per_bin = SBLK // unit_count
    bin_count = devices // groups_per_bin
    peer_blocks = MBLK // devices
    mic_units = bin_count * peer_blocks
    my_bin = device_id // groups_per_bin
    capacity = max(3, (2 * tile_count + devices - 1) // devices)
    slots = devices * capacity

    local_power = jnp.sum(jnp.square(plant.astype(jnp.float32)))
    header = jnp.concatenate([tile_pairs.astype(jnp.float32).reshape(-1), local_power[None]])
    headers = lax.all_gather(header, "spk")
    all_pairs = headers[:, : 2 * tile_count].reshape(devices, tile_count, 2).astype(jnp.int32)
    source_bin = jnp.arange(devices) // groups_per_bin
    bin_power = jnp.sum(jnp.where(source_bin == my_bin, headers[:, -1], 0.0))

    local_unit = tile_pairs[:, 0] % unit_count
    mic_block = tile_pairs[:, 1]
    target_peer = mic_block // peer_blocks
    position = target_peer * capacity + slot_ranks(target_peer, devices)
    send_onehot = position[None, :] == jnp.arange(slots)[:, None]

    peer_of = all_pairs[:, :, 1] // peer_blocks
    rank_of = slot_ranks(peer_of, devices)
    label_of = source_bin[:, None] * peer_blocks + all_pairs[:, :, 1] - device_id * peer_blocks
    mine = peer_of == device_id
    slot_hit = mine[:, :, None] & (rank_of[:, :, None] == jnp.arange(capacity))
    label_hit = label_of[:, :, None] == jnp.arange(mic_units)
    recv_onehot = jnp.einsum("stj,stm->msj", slot_hit.astype(jnp.float32),
                             label_hit.astype(jnp.float32)).reshape(mic_units, slots)

    direction_rows = direction.astype(jnp.bfloat16)[local_unit]
    partial_field = complex_forward(plant, direction_rows).astype(jnp.bfloat16)
    outgoing = select(send_onehot, partial_field).astype(jnp.bfloat16)
    arrived = lax.all_to_all(
        outgoing.reshape(devices, capacity, block_size, -1), "spk", 0, 0, tiled=True
    ).reshape(slots, block_size, -1)
    pressure = select(recv_onehot, arrived)
    weights_flat = mic_weight.reshape(mic_units, block_size)
    weighted = (weights_flat[:, :, None] * pressure).astype(jnp.bfloat16)

    reply = select(recv_onehot.T, weighted).astype(jnp.bfloat16)
    returned = lax.all_to_all(
        reply.reshape(devices, capacity, block_size, -1), "spk", 0, 0, tiled=True
    ).reshape(slots, block_size, -1)
    tile_weighted = select(send_onehot.T, returned).astype(jnp.bfloat16)
    back_field = complex_adjoint(plant, tile_weighted)
    unit_onehot = (local_unit[:, None] == jnp.arange(unit_count)[None, :]).astype(jnp.float32)
    gram = jnp.einsum("tu,tjk->ujk", unit_onehot, back_field, precision=lax.Precision.HIGHEST)
    return gram + reg_weight * bin_power / SPEAKERS * direction


def solution(mesh):
    placed = (
        P(("band", "spk"), None, None),
        P(("band", "spk"), None, None, None),
        P(("band", "spk"), None),
        P("band", "spk", None),
    )
    return jax.shard_map(
        per_device,
        mesh=mesh,
        in_specs=placed,
        out_specs=P(("band", "spk"), None, None),
        check_vma=False,
    )
```

```python
import jax
import jax.numpy as jnp
from jax import lax
from jax.sharding import PartitionSpec as P

SBLK = 32
MBLK = 128
SPEAKERS = 4096


reg_weight = 0.25


def complex_forward(plant, field_rows):
    halfway = field_rows.shape[-1] // 2
    product = jnp.einsum("tcij,tjk->tcik", plant, field_rows, preferred_element_type=jnp.float32)
    real_part = product[:, 0, :, :halfway] - product[:, 1, :, halfway:]
    imag_part = product[:, 0, :, halfway:] + product[:, 1, :, :halfway]
    return jnp.concatenate([real_part, imag_part], axis=-1)


def complex_adjoint(plant, field_rows):
    halfway = field_rows.shape[-1] // 2
    product = jnp.einsum("tcij,tik->tcjk", plant, field_rows, preferred_element_type=jnp.float32)
    real_part = product[:, 0, :, :halfway] + product[:, 1, :, halfway:]
    imag_part = product[:, 0, :, halfway:] - product[:, 1, :, :halfway]
    return jnp.concatenate([real_part, imag_part], axis=-1)


def slot_ranks(target_peer, devices):
    onehot = (target_peer[..., :, None] == jnp.arange(devices)).astype(jnp.int32)
    running = jnp.cumsum(onehot, axis=-2)
    return jnp.take_along_axis(running, target_peer[..., None], axis=-1)[..., 0] - 1


def per_device(direction, plant, tile_pairs, mic_weight):
    devices = lax.axis_size("spk")
    device_id = lax.axis_index("spk")
    unit_count = direction.shape[0]
    tile_count = plant.shape[0]
    block_size = direction.shape[1]
    field_width = direction.shape[2]
    groups_per_bin = SBLK // unit_count
    bin_count = devices // groups_per_bin
    peer_blocks = MBLK // devices
    mic_units = bin_count * peer_blocks
    my_bin = device_id // groups_per_bin
    capacity = max(3, (2 * tile_count + devices - 1) // devices)
    slots = devices * capacity

    local_power = jnp.sum(jnp.square(plant.astype(jnp.float32)))
    header = jnp.concatenate([tile_pairs.astype(jnp.float32).reshape(-1), local_power[None]])
    headers = lax.all_gather(header, "spk")
    headers, plant, direction = lax.optimization_barrier((headers, plant, direction))
    all_pairs = headers[:, : 2 * tile_count].reshape(devices, tile_count, 2).astype(jnp.int32)
    source_bin = jnp.arange(devices) // groups_per_bin
    bin_power = jnp.sum(jnp.where(source_bin == my_bin, headers[:, -1], 0.0))

    local_unit = tile_pairs[:, 0] % unit_count
    mic_block = tile_pairs[:, 1]
    target_peer = mic_block // peer_blocks
    position = target_peer * capacity + slot_ranks(target_peer, devices)
    send_hit = position[None, :] == jnp.arange(slots)[:, None]
    slot_pair = jnp.where(
        send_hit.any(axis=1), jnp.sum(jnp.where(send_hit, jnp.arange(tile_count), 0), axis=1), tile_count
    )

    peer_of = all_pairs[:, :, 1] // peer_blocks
    rank_of = slot_ranks(peer_of, devices)
    label_of = source_bin[:, None] * peer_blocks + all_pairs[:, :, 1] - device_id * peer_blocks
    slot_hit = (peer_of == device_id)[:, :, None] & (rank_of[:, :, None] == jnp.arange(capacity))
    slot_label = jnp.where(
        slot_hit.any(axis=1), jnp.sum(jnp.where(slot_hit, label_of[:, :, None], 0), axis=1), mic_units
    ).reshape(slots)
    recv_onehot = (slot_label[None, :] == jnp.arange(mic_units)[:, None]).astype(jnp.bfloat16)

    direction_rows = direction.astype(jnp.bfloat16)[local_unit]
    partial_field = complex_forward(plant, direction_rows).astype(jnp.bfloat16)
    outgoing = jnp.take(partial_field, slot_pair, axis=0, mode="fill", fill_value=0)
    arrived = lax.all_to_all(
        outgoing.reshape(devices, capacity * block_size, field_width), "spk", 0, 0, tiled=True
    ).reshape(slots, block_size, field_width)
    pressure = jnp.einsum("ms,sjk->mjk", recv_onehot, arrived, preferred_element_type=jnp.float32)
    weights_flat = mic_weight.reshape(mic_units, block_size)
    weighted = (weights_flat[:, :, None] * pressure).astype(jnp.bfloat16)

    reply = jnp.take(weighted, slot_label, axis=0, mode="fill", fill_value=0)
    returned = lax.all_to_all(
        reply.reshape(devices, capacity * block_size, field_width), "spk", 0, 0, tiled=True
    ).reshape(slots, block_size, field_width)
    tile_weighted = jnp.take(returned, position, axis=0)
    back_field = complex_adjoint(plant, tile_weighted)
    unit_onehot = (local_unit[:, None] == jnp.arange(unit_count)[None, :]).astype(jnp.float32)
    gram = jnp.einsum("tu,tjk->ujk", unit_onehot, back_field, precision=lax.Precision.HIGHEST)
    return gram + reg_weight * bin_power / SPEAKERS * direction


def solution(mesh):
    placed = (
        P(("band", "spk"), None, None),
        P(("band", "spk"), None, None, None),
        P(("band", "spk"), None),
        P("band", "spk", None),
    )
    return jax.shard_map(
        per_device,
        mesh=mesh,
        in_specs=placed,
        out_specs=P(("band", "spk"), None, None),
        check_vma=False,
    )
```

```python
import jax
import jax.numpy as jnp
from jax import lax
from jax.sharding import PartitionSpec as P

SBLK = 32
MBLK = 128
SPEAKERS = 4096


reg_weight = 0.25


def swap_halves(rows, sign):
    width = rows.shape[-1]
    half = width // 2
    col = jnp.arange(width)
    flip = ((col[:, None] + half) % width == col[None, :]).astype(rows.dtype)
    flip = flip * jnp.where(col[None, :] < half, -sign, sign).astype(rows.dtype)
    return jnp.einsum("...ik,kl->...il", rows, flip, preferred_element_type=jnp.float32).astype(rows.dtype)


def slot_ranks(target_peer, devices):
    onehot = (target_peer[..., :, None] == jnp.arange(devices)).astype(jnp.int32)
    running = jnp.cumsum(onehot, axis=-2)
    return jnp.take_along_axis(running, target_peer[..., None], axis=-1)[..., 0] - 1


def per_device(direction, plant, tile_pairs, mic_weight):
    devices = lax.axis_size("spk")
    device_id = lax.axis_index("spk")
    unit_count = direction.shape[0]
    tile_count = plant.shape[0]
    block_size = direction.shape[1]
    field_width = direction.shape[2]
    groups_per_bin = SBLK // unit_count
    bin_count = devices // groups_per_bin
    peer_blocks = MBLK // devices
    mic_units = bin_count * peer_blocks
    my_bin = device_id // groups_per_bin
    capacity = max(3, (2 * tile_count + devices - 1) // devices)
    slots = devices * capacity

    local_unit = tile_pairs[:, 0] % unit_count
    mic_block = tile_pairs[:, 1]
    target_peer = mic_block // peer_blocks
    position = target_peer * capacity + slot_ranks(target_peer, devices)
    send_hit = position[None, :] == jnp.arange(slots)[:, None]
    slot_pair = jnp.sum(jnp.where(send_hit, jnp.arange(tile_count), 0), axis=1)
    target_label = my_bin * peer_blocks + mic_block - target_peer * peer_blocks
    slot_label = jnp.where(
        send_hit.any(axis=1), jnp.sum(jnp.where(send_hit, target_label, 0), axis=1), mic_units
    )

    local_power = jnp.sum(jnp.square(plant.astype(jnp.float32)))
    header = jnp.concatenate(
        [slot_label.reshape(devices, capacity).astype(jnp.float32),
         jnp.broadcast_to(local_power, (devices, 1))], axis=1)
    header_in = lax.all_to_all(header, "spk", 0, 0, tiled=True)
    labels_in = header_in[:, :capacity].astype(jnp.int32).reshape(slots)
    source_bin = jnp.arange(devices) // groups_per_bin
    bin_power = jnp.sum(jnp.where(source_bin == my_bin, header_in[:, capacity], 0.0))
    recv_onehot = (labels_in[None, :] == jnp.arange(mic_units)[:, None]).astype(jnp.bfloat16)

    rounded = direction.astype(jnp.bfloat16)
    both = jnp.stack([rounded, swap_halves(rounded, 1)], axis=1)
    pair_rows = both[local_unit]
    partial_field = jnp.einsum("tcij,tcjk->tik", plant, pair_rows,
                               preferred_element_type=jnp.float32).astype(jnp.bfloat16)
    outgoing = jnp.take(partial_field, slot_pair, axis=0, mode="clip")
    arrived = lax.all_to_all(
        outgoing.reshape(devices, capacity * block_size, field_width), "spk", 0, 0, tiled=True
    ).reshape(slots, block_size, field_width)
    pressure = jnp.einsum("ms,sjk->mjk", recv_onehot, arrived, preferred_element_type=jnp.float32)
    weights_flat = mic_weight.reshape(mic_units, block_size)
    weighted = (weights_flat[:, :, None] * pressure).astype(jnp.bfloat16)

    reply = jnp.take(weighted, jnp.minimum(labels_in, mic_units - 1), axis=0, mode="clip")
    returned = lax.all_to_all(
        reply.reshape(devices, capacity * block_size, field_width), "spk", 0, 0, tiled=True
    ).reshape(slots, block_size, field_width)
    tile_weighted = jnp.take(returned, position, axis=0, mode="clip")

    back_rows = jnp.stack([tile_weighted, swap_halves(tile_weighted, -1)], axis=1)
    unit_mask = (local_unit[:, None] == jnp.arange(unit_count)[None, :]).astype(jnp.bfloat16)
    masked = back_rows[:, None] * unit_mask[:, :, None, None, None]
    gram = jnp.einsum("tcij,tucik->ujk", plant, masked, preferred_element_type=jnp.float32)
    return gram + reg_weight * bin_power / SPEAKERS * direction


def solution(mesh):
    placed = (
        P(("band", "spk"), None, None),
        P(("band", "spk"), None, None, None),
        P(("band", "spk"), None),
        P("band", "spk", None),
    )
    return jax.shard_map(
        per_device,
        mesh=mesh,
        in_specs=placed,
        out_specs=P(("band", "spk"), None, None),
        check_vma=False,
    )
```

```python
import jax
import jax.numpy as jnp
from jax import lax
from jax.sharding import PartitionSpec as P

SBLK = 32
MBLK = 128
SPEAKERS = 4096


reg_weight = 0.25


def swap_halves(rows, sign):
    width = rows.shape[-2]
    half = width // 2
    col = jnp.arange(width)
    flip = ((col[:, None] + half) % width == col[None, :]).astype(rows.dtype)
    flip = flip * jnp.where(col[None, :] < half, -sign, sign).astype(rows.dtype)
    return jnp.einsum("...ki,kl->...li", rows, flip, preferred_element_type=jnp.float32).astype(rows.dtype)


def slot_ranks(target_peer, devices):
    onehot = (target_peer[..., :, None] == jnp.arange(devices)).astype(jnp.int32)
    running = jnp.cumsum(onehot, axis=-2)
    return jnp.take_along_axis(running, target_peer[..., None], axis=-1)[..., 0] - 1


def with_header(blocks, values, devices, capacity):
    rows, lanes = blocks.shape[1], blocks.shape[2]
    body = blocks.reshape(devices, capacity * rows, lanes)
    head = jnp.pad(values.astype(blocks.dtype)[:, None, :], ((0, 0), (0, 15), (0, lanes - values.shape[1])))
    return jnp.concatenate([body, head], axis=1)


def split_header(buffer, capacity, rows, width):
    body = buffer[:, : capacity * rows].reshape(-1, rows, buffer.shape[2])
    return body, buffer[:, capacity * rows, :width]


def per_device(direction, plant, tile_pairs, mic_weight):
    devices = lax.axis_size("spk")
    device_id = lax.axis_index("spk")
    unit_count = direction.shape[0]
    tile_count = plant.shape[0]
    block_size = direction.shape[1]
    field_width = direction.shape[2]
    groups_per_bin = SBLK // unit_count
    bin_count = devices // groups_per_bin
    peer_blocks = MBLK // devices
    mic_units = bin_count * peer_blocks
    my_bin = device_id // groups_per_bin
    capacity = max(3, (2 * tile_count + devices - 1) // devices)
    slots = devices * capacity

    local_unit = tile_pairs[:, 0] % unit_count
    mic_block = tile_pairs[:, 1]
    target_peer = mic_block // peer_blocks
    position = target_peer * capacity + slot_ranks(target_peer, devices)
    send_hit = position[None, :] == jnp.arange(slots)[:, None]
    slot_pair = jnp.sum(jnp.where(send_hit, jnp.arange(tile_count), 0), axis=1)
    target_label = my_bin * peer_blocks + mic_block - target_peer * peer_blocks
    slot_label = jnp.where(
        send_hit.any(axis=1), jnp.sum(jnp.where(send_hit, target_label, 0), axis=1), mic_units
    )

    rounded = jnp.swapaxes(direction.astype(jnp.bfloat16), 1, 2)
    both = jnp.stack([rounded, swap_halves(rounded, 1)], axis=1)
    pair_rows = both[local_unit]
    partial_field = jnp.einsum("tcij,tckj->tki", plant, pair_rows,
                               preferred_element_type=jnp.float32).astype(jnp.bfloat16)
    outgoing = jnp.take(partial_field, slot_pair, axis=0, mode="clip")
    sent = with_header(outgoing, slot_label.reshape(devices, capacity), devices, capacity)
    arrived, labels_in = split_header(
        lax.all_to_all(sent, "spk", 0, 0, tiled=True), capacity, field_width, capacity)
    labels_in = labels_in.astype(jnp.int32).reshape(slots)
    recv_onehot = (labels_in[None, :] == jnp.arange(mic_units)[:, None]).astype(jnp.bfloat16)
    pressure = jnp.einsum("ms,ski->mki", recv_onehot, arrived, preferred_element_type=jnp.float32)
    weights_flat = mic_weight.reshape(mic_units, block_size)
    weighted = (weights_flat[:, None, :] * pressure).astype(jnp.bfloat16)

    local_power = jnp.sum(jnp.square(plant.astype(jnp.float32)))
    power_hi = local_power.astype(jnp.bfloat16).astype(jnp.float32)
    power_mid = (local_power - power_hi).astype(jnp.bfloat16).astype(jnp.float32)
    power_lo = local_power - power_hi - power_mid
    power_parts = jnp.broadcast_to(jnp.stack([power_hi, power_mid, power_lo]), (devices, 3))
    reply = jnp.take(weighted, jnp.minimum(labels_in, mic_units - 1), axis=0, mode="clip")
    returned, powers_in = split_header(
        lax.all_to_all(with_header(reply, power_parts, devices, capacity), "spk", 0, 0, tiled=True),
        capacity, field_width, 3)
    source_bin = jnp.arange(devices) // groups_per_bin
    power_of = jnp.sum(powers_in.astype(jnp.float32), axis=1)
    bin_power = jnp.sum(jnp.where(source_bin == my_bin, power_of, 0.0))
    tile_weighted = jnp.take(returned, position, axis=0, mode="clip")

    back_rows = jnp.stack([tile_weighted, swap_halves(tile_weighted, -1)], axis=1)
    unit_mask = (local_unit[:, None] == jnp.arange(unit_count)[None, :]).astype(jnp.bfloat16)
    masked = back_rows[:, None] * unit_mask[:, :, None, None, None]
    gram = jnp.einsum("tcij,tucki->ujk", plant, masked, preferred_element_type=jnp.float32)
    return gram + reg_weight * bin_power / SPEAKERS * direction


def solution(mesh):
    placed = (
        P(("band", "spk"), None, None),
        P(("band", "spk"), None, None, None),
        P(("band", "spk"), None),
        P("band", "spk", None),
    )
    return jax.shard_map(
        per_device,
        mesh=mesh,
        in_specs=placed,
        out_specs=P(("band", "spk"), None, None),
        check_vma=False,
    )
```

```python
import jax
import jax.numpy as jnp
from jax import lax
from jax.sharding import PartitionSpec as P

SBLK = 32
MBLK = 128
SPEAKERS = 4096


reg_weight = 0.25


def swap_halves(rows, sign):
    width = rows.shape[-2]
    half = width // 2
    col = jnp.arange(width)
    flip = ((col[:, None] + half) % width == col[None, :]).astype(rows.dtype)
    flip = flip * jnp.where(col[None, :] < half, -sign, sign).astype(rows.dtype)
    return jnp.einsum("...ki,kl->...li", rows, flip, preferred_element_type=jnp.float32).astype(rows.dtype)


def slot_ranks(target_peer, devices):
    onehot = (target_peer[..., :, None] == jnp.arange(devices)).astype(jnp.int32)
    running = jnp.cumsum(onehot, axis=-2)
    return jnp.take_along_axis(running, target_peer[..., None], axis=-1)[..., 0] - 1


def with_header(blocks, values, devices, capacity):
    rows, lanes = blocks.shape[1], blocks.shape[2]
    body = blocks.reshape(devices, capacity * rows, lanes)
    head = jnp.pad(values.astype(blocks.dtype)[:, None, :], ((0, 0), (0, 15), (0, lanes - values.shape[1])))
    return jnp.concatenate([body, head], axis=1)


def split_header(buffer, capacity, rows, width):
    body = buffer[:, : capacity * rows].reshape(-1, rows, buffer.shape[2])
    return body, buffer[:, capacity * rows, :width]


def per_device(direction, plant, tile_pairs, mic_weight):
    devices = lax.axis_size("spk")
    device_id = lax.axis_index("spk")
    unit_count = direction.shape[0]
    tile_count = plant.shape[0]
    block_size = direction.shape[1]
    field_width = direction.shape[2]
    groups_per_bin = SBLK // unit_count
    bin_count = devices // groups_per_bin
    peer_blocks = MBLK // devices
    mic_units = bin_count * peer_blocks
    my_bin = device_id // groups_per_bin
    capacity = max(3, (2 * tile_count + devices - 1) // devices)
    slots = devices * capacity

    local_unit = tile_pairs[:, 0] % unit_count
    mic_block = tile_pairs[:, 1]
    target_peer = mic_block // peer_blocks
    position = target_peer * capacity + slot_ranks(target_peer, devices)
    send_hit = position[None, :] == jnp.arange(slots)[:, None]
    slot_pair = jnp.sum(jnp.where(send_hit, jnp.arange(tile_count), 0), axis=1)
    target_label = my_bin * peer_blocks + mic_block - target_peer * peer_blocks
    slot_label = jnp.where(
        send_hit.any(axis=1), jnp.sum(jnp.where(send_hit, target_label, 0), axis=1), mic_units
    )

    rounded = jnp.swapaxes(direction.astype(jnp.bfloat16), 1, 2)
    both = jnp.stack([rounded, swap_halves(rounded, 1)], axis=1)
    pair_rows = both[local_unit]
    partial_field = jnp.einsum("tcij,tckj->tki", plant, pair_rows,
                               preferred_element_type=jnp.float32).astype(jnp.bfloat16)
    outgoing = jnp.take(partial_field, slot_pair, axis=0, mode="clip")
    sent = with_header(outgoing, slot_label.reshape(devices, capacity), devices, capacity)
    arrived, labels_in = split_header(
        lax.all_to_all(sent, "spk", 0, 0, tiled=True), capacity, field_width, capacity)
    labels_in = labels_in.astype(jnp.int32).reshape(slots)
    recv_onehot = (labels_in[None, :] == jnp.arange(mic_units)[:, None]).astype(jnp.bfloat16)
    pressure = jnp.einsum("ms,ski->mki", recv_onehot, arrived, preferred_element_type=jnp.float32)
    weights_flat = mic_weight.reshape(mic_units, block_size)
    weighted = (weights_flat[:, None, :] * pressure).astype(jnp.bfloat16)

    local_power = jnp.sum(jnp.square(plant.astype(jnp.float32)))
    power_hi = local_power.astype(jnp.bfloat16).astype(jnp.float32)
    power_mid = (local_power - power_hi).astype(jnp.bfloat16).astype(jnp.float32)
    power_lo = local_power - power_hi - power_mid
    power_parts = jnp.stack([power_hi, power_mid, power_lo])[None, :]
    shared = with_header(weighted, power_parts, 1, mic_units)[0]
    gathered = lax.all_gather(shared, "spk")
    source_bin = jnp.arange(devices) // groups_per_bin
    power_of = jnp.sum(gathered[:, mic_units * field_width, :3].astype(jnp.float32), axis=1)
    bin_power = jnp.sum(jnp.where(source_bin == my_bin, power_of, 0.0))
    tile_weighted = jax.vmap(
        lambda peer, row: lax.dynamic_slice(gathered, (peer, row, 0), (1, field_width, block_size))[0]
    )(target_peer, target_label * field_width)

    back_rows = jnp.stack([tile_weighted, swap_halves(tile_weighted, -1)], axis=1)
    unit_mask = (local_unit[:, None] == jnp.arange(unit_count)[None, :]).astype(jnp.bfloat16)
    masked = back_rows[:, None] * unit_mask[:, :, None, None, None]
    gram = jnp.einsum("tcij,tucki->ujk", plant, masked, preferred_element_type=jnp.float32)
    return gram + reg_weight * bin_power / SPEAKERS * direction


def solution(mesh):
    placed = (
        P(("band", "spk"), None, None),
        P(("band", "spk"), None, None, None),
        P(("band", "spk"), None),
        P("band", "spk", None),
    )
    return jax.shard_map(
        per_device,
        mesh=mesh,
        in_specs=placed,
        out_specs=P(("band", "spk"), None, None),
        check_vma=False,
    )
```

```python
import jax
import jax.numpy as jnp
from jax import lax
from jax.sharding import PartitionSpec as P

SBLK = 32
MBLK = 128
SPEAKERS = 4096


reg_weight = 0.25


def swap_halves(rows, sign):
    width = rows.shape[-2]
    half = width // 2
    col = jnp.arange(width)
    flip = ((col[:, None] + half) % width == col[None, :]).astype(rows.dtype)
    flip = flip * jnp.where(col[None, :] < half, -sign, sign).astype(rows.dtype)
    return jnp.einsum("...ki,kl->...li", rows, flip, preferred_element_type=jnp.float32).astype(rows.dtype)


def slot_ranks(target_peer, devices):
    onehot = (target_peer[..., :, None] == jnp.arange(devices)).astype(jnp.int32)
    running = jnp.cumsum(onehot, axis=-2)
    return jnp.take_along_axis(running, target_peer[..., None], axis=-1)[..., 0] - 1


def with_header(blocks, values, devices, capacity):
    rows, lanes = blocks.shape[1], blocks.shape[2]
    body = blocks.reshape(devices, capacity * rows, lanes)
    head = jnp.pad(values.astype(blocks.dtype)[:, None, :], ((0, 0), (0, 15), (0, lanes - values.shape[1])))
    return jnp.concatenate([body, head], axis=1)


def split_header(buffer, capacity, rows, width):
    body = buffer[:, : capacity * rows].reshape(-1, rows, buffer.shape[2])
    return body, buffer[:, capacity * rows, :width]


def per_device(direction, plant, tile_pairs, mic_weight):
    devices = lax.axis_size("spk")
    device_id = lax.axis_index("spk")
    unit_count = direction.shape[0]
    tile_count = plant.shape[0]
    block_size = direction.shape[1]
    field_width = direction.shape[2]
    groups_per_bin = SBLK // unit_count
    bin_count = devices // groups_per_bin
    peer_blocks = MBLK // devices
    mic_units = bin_count * peer_blocks
    my_bin = device_id // groups_per_bin
    capacity = max(3, (2 * tile_count + devices - 1) // devices)
    slots = devices * capacity

    local_unit = tile_pairs[:, 0] % unit_count
    mic_block = tile_pairs[:, 1]
    target_peer = mic_block // peer_blocks
    position = target_peer * capacity + slot_ranks(target_peer, devices)
    send_hit = position[None, :] == jnp.arange(slots)[:, None]
    slot_pair = jnp.sum(jnp.where(send_hit, jnp.arange(tile_count), 0), axis=1)
    target_label = my_bin * peer_blocks + mic_block - target_peer * peer_blocks
    slot_label = jnp.where(
        send_hit.any(axis=1), jnp.sum(jnp.where(send_hit, target_label, 0), axis=1), mic_units
    )

    chunks = 2
    fields = field_width // 2
    per_chunk = fields // chunks
    rounded = jnp.swapaxes(direction.astype(jnp.bfloat16), 1, 2)
    weights_flat = mic_weight.reshape(mic_units, block_size)
    unit_mask = (local_unit[:, None] == jnp.arange(unit_count)[None, :]).astype(jnp.bfloat16)
    local_power = jnp.sum(jnp.square(plant.astype(jnp.float32)))
    power_hi = local_power.astype(jnp.bfloat16).astype(jnp.float32)
    power_mid = (local_power - power_hi).astype(jnp.bfloat16).astype(jnp.float32)
    power_lo = local_power - power_hi - power_mid
    power_parts = jnp.broadcast_to(jnp.stack([power_hi, power_mid, power_lo]), (devices, 3))
    source_bin = jnp.arange(devices) // groups_per_bin

    labels_in = None
    bin_power = None
    real_parts, imag_parts = [], []
    for chunk in range(chunks):
        lo = chunk * per_chunk
        cols = jnp.concatenate([rounded[:, lo:lo + per_chunk], rounded[:, fields + lo:fields + lo + per_chunk]], axis=1)
        width = 2 * per_chunk
        both = jnp.stack([cols, swap_halves(cols, 1)], axis=1)
        pair_rows = both[local_unit]
        partial_field = jnp.einsum("tcij,tckj->tki", plant, pair_rows,
                                   preferred_element_type=jnp.float32).astype(jnp.bfloat16)
        outgoing = jnp.take(partial_field, slot_pair, axis=0, mode="clip")
        if chunk == 0:
            sent = with_header(outgoing, slot_label.reshape(devices, capacity), devices, capacity)
            arrived, header_in = split_header(
                lax.all_to_all(sent, "spk", 0, 0, tiled=True), capacity, width, capacity)
            labels_in = header_in.astype(jnp.int32).reshape(slots)
        else:
            arrived = lax.all_to_all(
                outgoing.reshape(devices, capacity * width, block_size), "spk", 0, 0, tiled=True
            ).reshape(slots, width, block_size)
        recv_onehot = (labels_in[None, :] == jnp.arange(mic_units)[:, None]).astype(jnp.bfloat16)
        pressure = jnp.einsum("ms,ski->mki", recv_onehot, arrived, preferred_element_type=jnp.float32)
        weighted = (weights_flat[:, None, :] * pressure).astype(jnp.bfloat16)

        reply = jnp.take(weighted, jnp.minimum(labels_in, mic_units - 1), axis=0, mode="clip")
        if chunk == 0:
            returned, powers_in = split_header(
                lax.all_to_all(with_header(reply, power_parts, devices, capacity), "spk", 0, 0, tiled=True),
                capacity, width, 3)
            power_of = jnp.sum(powers_in.astype(jnp.float32), axis=1)
            bin_power = jnp.sum(jnp.where(source_bin == my_bin, power_of, 0.0))
        else:
            returned = lax.all_to_all(
                reply.reshape(devices, capacity * width, block_size), "spk", 0, 0, tiled=True
            ).reshape(slots, width, block_size)
        tile_weighted = jnp.take(returned, position, axis=0, mode="clip")

        back_rows = jnp.stack([tile_weighted, swap_halves(tile_weighted, -1)], axis=1)
        masked = back_rows[:, None] * unit_mask[:, :, None, None, None]
        gram = jnp.einsum("tcij,tucki->ujk", plant, masked, preferred_element_type=jnp.float32)
        real_parts.append(gram[..., :per_chunk])
        imag_parts.append(gram[..., per_chunk:])
    gram = jnp.concatenate(real_parts + imag_parts, axis=-1)
    return gram + reg_weight * bin_power / SPEAKERS * direction


def solution(mesh):
    placed = (
        P(("band", "spk"), None, None),
        P(("band", "spk"), None, None, None),
        P(("band", "spk"), None),
        P("band", "spk", None),
    )
    return jax.shard_map(
        per_device,
        mesh=mesh,
        in_specs=placed,
        out_specs=P(("band", "spk"), None, None),
        check_vma=False,
    )
```

```python
import jax
import jax.numpy as jnp
from jax import lax
from jax.sharding import PartitionSpec as P

SBLK = 32
MBLK = 128
SPEAKERS = 4096


reg_weight = 0.25


def swap_halves(rows, sign):
    width = rows.shape[-2]
    half = width // 2
    col = jnp.arange(width)
    flip = ((col[:, None] + half) % width == col[None, :]).astype(rows.dtype)
    flip = flip * jnp.where(col[None, :] < half, -sign, sign).astype(rows.dtype)
    return jnp.einsum("...ki,kl->...li", rows, flip, preferred_element_type=jnp.float32).astype(rows.dtype)


def slot_ranks(target_peer, devices):
    onehot = (target_peer[..., :, None] == jnp.arange(devices)).astype(jnp.int32)
    running = jnp.cumsum(onehot, axis=-2)
    return jnp.take_along_axis(running, target_peer[..., None], axis=-1)[..., 0] - 1


def with_header(blocks, values, devices, capacity):
    rows, lanes = blocks.shape[1], blocks.shape[2]
    body = blocks.reshape(devices, capacity * rows, lanes)
    head = jnp.pad(values.astype(blocks.dtype)[:, None, :], ((0, 0), (0, 15), (0, lanes - values.shape[1])))
    return jnp.concatenate([body, head], axis=1)


def split_header(buffer, capacity, rows, width):
    body = buffer[:, : capacity * rows].reshape(-1, rows, buffer.shape[2])
    return body, buffer[:, capacity * rows, :width]


def per_device(direction, plant, tile_pairs, mic_weight):
    devices = lax.axis_size("spk")
    device_id = lax.axis_index("spk")
    unit_count = direction.shape[0]
    tile_count = plant.shape[0]
    block_size = direction.shape[1]
    field_width = direction.shape[2]
    groups_per_bin = SBLK // unit_count
    bin_count = devices // groups_per_bin
    peer_blocks = MBLK // devices
    mic_units = bin_count * peer_blocks
    my_bin = device_id // groups_per_bin
    capacity = max(3, (2 * tile_count + devices - 1) // devices)
    slots = devices * capacity

    local_unit = tile_pairs[:, 0] % unit_count
    mic_block = tile_pairs[:, 1]
    target_peer = mic_block // peer_blocks
    position = target_peer * capacity + slot_ranks(target_peer, devices)
    send_hit = position[None, :] == jnp.arange(slots)[:, None]
    slot_pair = jnp.sum(jnp.where(send_hit, jnp.arange(tile_count), 0), axis=1)
    target_label = my_bin * peer_blocks + mic_block - target_peer * peer_blocks
    slot_label = jnp.where(
        send_hit.any(axis=1), jnp.sum(jnp.where(send_hit, target_label, 0), axis=1), mic_units
    )

    rounded = jnp.swapaxes(direction.astype(jnp.bfloat16), 1, 2)
    both = jnp.stack([rounded, swap_halves(rounded, 1)], axis=1)
    pair_rows = both[local_unit]
    partial_field = jnp.einsum("tcij,tckj->tki", plant, pair_rows,
                               preferred_element_type=jnp.float32).astype(jnp.bfloat16)
    outgoing = jnp.take(partial_field, slot_pair, axis=0, mode="clip")
    squares = jnp.square(plant.astype(jnp.float32)).reshape(-1, block_size)
    local_power = jnp.sum(jnp.sum(squares, axis=0))
    power_hi = local_power.astype(jnp.bfloat16).astype(jnp.float32)
    power_mid = (local_power - power_hi).astype(jnp.bfloat16).astype(jnp.float32)
    power_lo = local_power - power_hi - power_mid
    power_parts = jnp.broadcast_to(jnp.stack([power_hi, power_mid, power_lo]), (devices, 3))
    header = jnp.concatenate([slot_label.reshape(devices, capacity).astype(jnp.float32), power_parts], axis=1)
    sent = with_header(outgoing, header, devices, capacity)
    arrived, header_in = split_header(
        lax.all_to_all(sent, "spk", 0, 0, tiled=True), capacity, field_width, capacity + 3)
    labels_in = header_in[:, :capacity].astype(jnp.int32).reshape(slots)
    source_bin = jnp.arange(devices) // groups_per_bin
    power_of = jnp.sum(header_in[:, capacity:].astype(jnp.float32), axis=1)
    bin_power = jnp.sum(jnp.where(source_bin == my_bin, power_of, 0.0))
    recv_onehot = (labels_in[None, :] == jnp.arange(mic_units)[:, None]).astype(jnp.bfloat16)
    pressure = jnp.einsum("ms,ski->mki", recv_onehot, arrived, preferred_element_type=jnp.float32)
    weights_flat = mic_weight.reshape(mic_units, block_size)
    weighted = (weights_flat[:, None, :] * pressure).astype(jnp.bfloat16)

    reply = jnp.take(weighted, jnp.minimum(labels_in, mic_units - 1), axis=0, mode="clip")
    returned = lax.all_to_all(
        reply.reshape(devices, capacity * field_width, block_size), "spk", 0, 0, tiled=True
    ).reshape(slots, field_width, block_size)
    tile_weighted = jnp.take(returned, position, axis=0, mode="clip")

    back_rows = jnp.stack([tile_weighted, swap_halves(tile_weighted, -1)], axis=1)
    unit_mask = (local_unit[:, None] == jnp.arange(unit_count)[None, :]).astype(jnp.bfloat16)
    masked = back_rows[:, None] * unit_mask[:, :, None, None, None]
    gram = jnp.einsum("tcij,tucki->ujk", plant, masked, preferred_element_type=jnp.float32)
    return gram + reg_weight * bin_power / SPEAKERS * direction


def solution(mesh):
    placed = (
        P(("band", "spk"), None, None),
        P(("band", "spk"), None, None, None),
        P(("band", "spk"), None),
        P("band", "spk", None),
    )
    return jax.shard_map(
        per_device,
        mesh=mesh,
        in_specs=placed,
        out_specs=P(("band", "spk"), None, None),
        check_vma=False,
    )
```

```python
import jax
import jax.numpy as jnp
from jax import lax
from jax.sharding import PartitionSpec as P

SBLK = 32
MBLK = 128
SPEAKERS = 4096


reg_weight = 0.25


def swap_halves(rows, sign):
    width = rows.shape[-2]
    half = width // 2
    col = jnp.arange(width)
    flip = ((col[:, None] + half) % width == col[None, :]).astype(rows.dtype)
    flip = flip * jnp.where(col[None, :] < half, -sign, sign).astype(rows.dtype)
    return jnp.einsum("...ki,kl->...li", rows, flip, preferred_element_type=jnp.float32).astype(rows.dtype)


def slot_ranks(target_peer, devices):
    onehot = (target_peer[..., :, None] == jnp.arange(devices)).astype(jnp.int32)
    running = jnp.cumsum(onehot, axis=-2)
    return jnp.take_along_axis(running, target_peer[..., None], axis=-1)[..., 0] - 1


def with_header(blocks, values, devices, capacity):
    rows, lanes = blocks.shape[1], blocks.shape[2]
    body = blocks.reshape(devices, capacity * rows, lanes)
    head = jnp.pad(values.astype(blocks.dtype)[:, None, :], ((0, 0), (0, 15), (0, lanes - values.shape[1])))
    return jnp.concatenate([body, head], axis=1)


def split_header(buffer, capacity, rows, width):
    body = buffer[:, : capacity * rows].reshape(-1, rows, buffer.shape[2])
    return body, buffer[:, capacity * rows, :width]


def per_device(direction, plant, tile_pairs, mic_weight):
    devices = lax.axis_size("spk")
    device_id = lax.axis_index("spk")
    unit_count = direction.shape[0]
    tile_count = plant.shape[0]
    block_size = direction.shape[1]
    field_width = direction.shape[2]
    groups_per_bin = SBLK // unit_count
    bin_count = devices // groups_per_bin
    peer_blocks = MBLK // devices
    mic_units = bin_count * peer_blocks
    my_bin = device_id // groups_per_bin
    capacity = max(3, (2 * tile_count + devices - 1) // devices)
    slots = devices * capacity

    local_unit = tile_pairs[:, 0] % unit_count
    mic_block = tile_pairs[:, 1]
    target_peer = mic_block // peer_blocks
    position = target_peer * capacity + slot_ranks(target_peer, devices)
    send_hit = position[None, :] == jnp.arange(slots)[:, None]
    slot_pair = jnp.sum(jnp.where(send_hit, jnp.arange(tile_count), 0), axis=1)
    target_label = my_bin * peer_blocks + mic_block - target_peer * peer_blocks
    slot_label = jnp.where(
        send_hit.any(axis=1), jnp.sum(jnp.where(send_hit, target_label, 0), axis=1), mic_units
    )

    rounded = jnp.swapaxes(direction.astype(jnp.bfloat16), 1, 2)
    both = jnp.stack([rounded, swap_halves(rounded, 1)], axis=1)
    pair_rows = both[local_unit]
    partial_field = jnp.einsum("tcij,tckj->tki", plant, pair_rows,
                               preferred_element_type=jnp.float32).astype(jnp.bfloat16)
    outgoing = jnp.take(partial_field, slot_pair, axis=0, mode="clip")
    plant_rows = plant.reshape(-1, block_size)
    local_power = jnp.trace(jnp.einsum("mj,mk->jk", plant_rows, plant_rows,
                                       preferred_element_type=jnp.float32))
    power_hi = local_power.astype(jnp.bfloat16).astype(jnp.float32)
    power_mid = (local_power - power_hi).astype(jnp.bfloat16).astype(jnp.float32)
    power_lo = local_power - power_hi - power_mid
    power_parts = jnp.broadcast_to(jnp.stack([power_hi, power_mid, power_lo]), (devices, 3))
    header = jnp.concatenate([slot_label.reshape(devices, capacity).astype(jnp.float32), power_parts], axis=1)
    sent = with_header(outgoing, header, devices, capacity)
    arrived, header_in = split_header(
        lax.all_to_all(sent, "spk", 0, 0, tiled=True), capacity, field_width, capacity + 3)
    labels_in = header_in[:, :capacity].astype(jnp.int32).reshape(slots)
    source_bin = jnp.arange(devices) // groups_per_bin
    power_of = jnp.sum(header_in[:, capacity:].astype(jnp.float32), axis=1)
    bin_power = jnp.sum(jnp.where(source_bin == my_bin, power_of, 0.0))
    valid = labels_in < mic_units
    same_unit = ((labels_in[:, None] == labels_in[None, :]) & valid[None, :]).astype(jnp.bfloat16)
    pressure = jnp.einsum("rs,ski->rki", same_unit, arrived, preferred_element_type=jnp.float32)
    weights_flat = mic_weight.reshape(mic_units, block_size)
    slot_weights = jnp.take(weights_flat, jnp.minimum(labels_in, mic_units - 1), axis=0)

    reply = (slot_weights[:, None, :] * pressure).astype(jnp.bfloat16)
    returned = lax.all_to_all(
        reply.reshape(devices, capacity * field_width, block_size), "spk", 0, 0, tiled=True
    ).reshape(slots, field_width, block_size)
    tile_weighted = jnp.take(returned, position, axis=0, mode="clip")

    back_rows = jnp.stack([tile_weighted, swap_halves(tile_weighted, -1)], axis=1)
    unit_mask = (local_unit[:, None] == jnp.arange(unit_count)[None, :]).astype(jnp.bfloat16)
    masked = back_rows[:, None] * unit_mask[:, :, None, None, None]
    gram = jnp.einsum("tcij,tucki->ujk", plant, masked, preferred_element_type=jnp.float32)
    return gram + reg_weight * bin_power / SPEAKERS * direction


def solution(mesh):
    placed = (
        P(("band", "spk"), None, None),
        P(("band", "spk"), None, None, None),
        P(("band", "spk"), None),
        P("band", "spk", None),
    )
    return jax.shard_map(
        per_device,
        mesh=mesh,
        in_specs=placed,
        out_specs=P(("band", "spk"), None, None),
        check_vma=False,
    )
```

```python
import jax
import jax.numpy as jnp
from jax import lax
from jax.sharding import PartitionSpec as P

SBLK = 32
MBLK = 128
SPEAKERS = 4096


reg_weight = 0.25


def swap_halves(rows, sign):
    width = rows.shape[-2]
    half = width // 2
    col = jnp.arange(width)
    flip = ((col[:, None] + half) % width == col[None, :]).astype(rows.dtype)
    flip = flip * jnp.where(col[None, :] < half, -sign, sign).astype(rows.dtype)
    return jnp.einsum("...ki,kl->...li", rows, flip, preferred_element_type=jnp.float32).astype(rows.dtype)


def slot_ranks(target_peer, devices):
    onehot = (target_peer[..., :, None] == jnp.arange(devices)).astype(jnp.int32)
    running = jnp.cumsum(onehot, axis=-2)
    return jnp.take_along_axis(running, target_peer[..., None], axis=-1)[..., 0] - 1


def with_header(blocks, values, devices, capacity):
    rows, lanes = blocks.shape[1], blocks.shape[2]
    body = blocks.reshape(devices, capacity * rows, lanes)
    head = jnp.pad(values.astype(blocks.dtype)[:, None, :], ((0, 0), (0, 15), (0, lanes - values.shape[1])))
    return jnp.concatenate([body, head], axis=1)


def split_header(buffer, capacity, rows, width):
    body = buffer[:, : capacity * rows].reshape(-1, rows, buffer.shape[2])
    return body, buffer[:, capacity * rows, :width]


def per_device(direction, plant, tile_pairs, mic_weight):
    devices = lax.axis_size("spk")
    device_id = lax.axis_index("spk")
    unit_count = direction.shape[0]
    tile_count = plant.shape[0]
    block_size = direction.shape[1]
    field_width = direction.shape[2]
    groups_per_bin = SBLK // unit_count
    bin_count = devices // groups_per_bin
    peer_blocks = MBLK // devices
    mic_units = bin_count * peer_blocks
    my_bin = device_id // groups_per_bin
    capacity = max(3, (2 * tile_count + devices - 1) // devices)
    slots = devices * capacity

    local_unit = tile_pairs[:, 0] % unit_count
    mic_block = tile_pairs[:, 1]
    target_peer = mic_block // peer_blocks
    position = target_peer * capacity + slot_ranks(target_peer, devices)
    send_hit = position[None, :] == jnp.arange(slots)[:, None]
    slot_pair = jnp.sum(jnp.where(send_hit, jnp.arange(tile_count), 0), axis=1)
    target_label = my_bin * peer_blocks + mic_block - target_peer * peer_blocks
    slot_label = jnp.where(
        send_hit.any(axis=1), jnp.sum(jnp.where(send_hit, target_label, 0), axis=1), mic_units
    )

    rounded = jnp.swapaxes(direction.astype(jnp.bfloat16), 1, 2)
    both = jnp.stack([rounded, swap_halves(rounded, 1)], axis=1)
    pair_rows = both[local_unit]
    partial_field = jnp.einsum("tcij,tckj->tki", plant, pair_rows,
                               preferred_element_type=jnp.float32).astype(jnp.bfloat16)
    outgoing = jnp.take(partial_field, slot_pair, axis=0, mode="clip")
    plant_rows = plant.reshape(-1, block_size)
    local_power = jnp.trace(jnp.einsum("mj,mk->jk", plant_rows, plant_rows,
                                       preferred_element_type=jnp.float32))
    power_hi = local_power.astype(jnp.bfloat16).astype(jnp.float32)
    power_mid = (local_power - power_hi).astype(jnp.bfloat16).astype(jnp.float32)
    power_lo = local_power - power_hi - power_mid
    power_parts = jnp.broadcast_to(jnp.stack([power_hi, power_mid, power_lo]), (devices, 3))
    header = jnp.concatenate([slot_label.reshape(devices, capacity).astype(jnp.float32), power_parts], axis=1)
    sent = with_header(outgoing, header, devices, capacity)
    arrived, header_in = split_header(
        lax.all_to_all(sent, "spk", 0, 0, tiled=True), capacity, field_width, capacity + 3)
    labels_in = header_in[:, :capacity].astype(jnp.int32).reshape(slots)
    source_bin = jnp.arange(devices) // groups_per_bin
    power_of = jnp.sum(header_in[:, capacity:].astype(jnp.float32), axis=1)
    bin_power = jnp.sum(jnp.where(source_bin == my_bin, power_of, 0.0))
    recv_onehot = (labels_in[None, :] == jnp.arange(mic_units)[:, None]).astype(jnp.bfloat16)
    pressure = jnp.einsum("ms,ski->mki", recv_onehot, arrived, preferred_element_type=jnp.float32)
    weights_flat = mic_weight.reshape(mic_units, block_size)
    weighted = (weights_flat[:, None, :] * pressure).astype(jnp.bfloat16)

    reply = jnp.take(weighted, jnp.minimum(labels_in, mic_units - 1), axis=0, mode="clip")
    returned = lax.all_to_all(
        reply.reshape(devices, capacity * field_width, block_size), "spk", 0, 0, tiled=True
    ).reshape(slots, field_width, block_size)
    tile_weighted = jnp.take(returned, position, axis=0, mode="clip")

    back_rows = jnp.stack([tile_weighted, swap_halves(tile_weighted, -1)], axis=1)
    unit_mask = (local_unit[:, None] == jnp.arange(unit_count)[None, :]).astype(jnp.bfloat16)
    masked = back_rows[:, None] * unit_mask[:, :, None, None, None]
    gram = jnp.einsum("tcij,tucki->ujk", plant, masked, preferred_element_type=jnp.float32)
    return gram + reg_weight * bin_power / SPEAKERS * direction


def solution(mesh):
    placed = (
        P(("band", "spk"), None, None),
        P(("band", "spk"), None, None, None),
        P(("band", "spk"), None),
        P("band", "spk", None),
    )
    return jax.shard_map(
        per_device,
        mesh=mesh,
        in_specs=placed,
        out_specs=P(("band", "spk"), None, None),
        check_vma=False,
    )
```

```python
import jax
import jax.numpy as jnp
from jax import lax
from jax.sharding import PartitionSpec as P

SBLK = 32
MBLK = 128
SPEAKERS = 4096


reg_weight = 0.25


def swap_halves(rows, sign):
    width = rows.shape[-2]
    half = width // 2
    col = jnp.arange(width)
    flip = ((col[:, None] + half) % width == col[None, :]).astype(rows.dtype)
    flip = flip * jnp.where(col[None, :] < half, -sign, sign).astype(rows.dtype)
    return jnp.einsum("...ki,kl->...li", rows, flip, preferred_element_type=jnp.float32).astype(rows.dtype)


def slot_ranks(target_peer, devices):
    onehot = (target_peer[..., :, None] == jnp.arange(devices)).astype(jnp.int32)
    running = jnp.cumsum(onehot, axis=-2)
    return jnp.take_along_axis(running, target_peer[..., None], axis=-1)[..., 0] - 1


def with_header(blocks, values, devices, capacity):
    rows, lanes = blocks.shape[1], blocks.shape[2]
    body = blocks.reshape(devices, capacity * rows, lanes)
    head = jnp.pad(values.astype(blocks.dtype)[:, None, :], ((0, 0), (0, 15), (0, lanes - values.shape[1])))
    return jnp.concatenate([body, head], axis=1)


def split_header(buffer, capacity, rows, width):
    body = buffer[:, : capacity * rows].reshape(-1, rows, buffer.shape[2])
    return body, buffer[:, capacity * rows, :width]


def per_device(direction, plant, tile_pairs, mic_weight):
    devices = lax.axis_size("spk")
    device_id = lax.axis_index("spk")
    unit_count = direction.shape[0]
    tile_count = plant.shape[0]
    block_size = direction.shape[1]
    field_width = direction.shape[2]
    groups_per_bin = SBLK // unit_count
    bin_count = devices // groups_per_bin
    peer_blocks = MBLK // devices
    mic_units = bin_count * peer_blocks
    my_bin = device_id // groups_per_bin
    capacity = max(3, (2 * tile_count + devices - 1) // devices)
    slots = devices * capacity

    local_unit = tile_pairs[:, 0] % unit_count
    mic_block = tile_pairs[:, 1]
    target_peer = mic_block // peer_blocks
    position = target_peer * capacity + slot_ranks(target_peer, devices)
    send_hit = position[None, :] == jnp.arange(slots)[:, None]
    slot_pair = jnp.sum(jnp.where(send_hit, jnp.arange(tile_count), 0), axis=1)
    target_label = my_bin * peer_blocks + mic_block - target_peer * peer_blocks
    slot_label = jnp.where(
        send_hit.any(axis=1), jnp.sum(jnp.where(send_hit, target_label, 0), axis=1), mic_units
    )

    rounded = jnp.swapaxes(direction.astype(jnp.bfloat16), 1, 2)
    both = jnp.stack([rounded, swap_halves(rounded, 1)], axis=1)
    pair_rows = both[local_unit]
    partial_field = jnp.einsum("tcij,tckj->tki", plant, pair_rows,
                               preferred_element_type=jnp.float32).astype(jnp.bfloat16)
    outgoing = jnp.take(partial_field, slot_pair, axis=0, mode="clip")
    local_power = jnp.trace(jnp.einsum("tcij,tcik->jk", plant, plant,
                                       preferred_element_type=jnp.float32))
    power_hi = local_power.astype(jnp.bfloat16).astype(jnp.float32)
    power_mid = (local_power - power_hi).astype(jnp.bfloat16).astype(jnp.float32)
    power_lo = local_power - power_hi - power_mid
    power_parts = jnp.broadcast_to(jnp.stack([power_hi, power_mid, power_lo]), (devices, 3))
    header = jnp.concatenate([slot_label.reshape(devices, capacity).astype(jnp.float32), power_parts], axis=1)
    sent = with_header(outgoing, header, devices, capacity)
    arrived, header_in = split_header(
        lax.all_to_all(sent, "spk", 0, 0, tiled=True), capacity, field_width, capacity + 3)
    labels_in = header_in[:, :capacity].astype(jnp.int32).reshape(slots)
    source_bin = jnp.arange(devices) // groups_per_bin
    power_of = jnp.sum(header_in[:, capacity:].astype(jnp.float32), axis=1)
    bin_power = jnp.sum(jnp.where(source_bin == my_bin, power_of, 0.0))
    recv_onehot = (labels_in[None, :] == jnp.arange(mic_units)[:, None]).astype(jnp.bfloat16)
    pressure = jnp.einsum("ms,ski->mki", recv_onehot, arrived, preferred_element_type=jnp.float32)
    weights_flat = mic_weight.reshape(mic_units, block_size)
    weighted = (weights_flat[:, None, :] * pressure).astype(jnp.bfloat16)

    reply = jnp.take(weighted, jnp.minimum(labels_in, mic_units - 1), axis=0, mode="clip")
    returned = lax.all_to_all(
        reply.reshape(devices, capacity * field_width, block_size), "spk", 0, 0, tiled=True
    ).reshape(slots, field_width, block_size)
    tile_weighted = jnp.take(returned, position, axis=0, mode="clip")

    back_rows = jnp.stack([tile_weighted, swap_halves(tile_weighted, -1)], axis=1)
    unit_mask = (local_unit[:, None] == jnp.arange(unit_count)[None, :]).astype(jnp.bfloat16)
    masked = back_rows[:, None] * unit_mask[:, :, None, None, None]
    gram = jnp.einsum("tcij,tucki->ujk", plant, masked, preferred_element_type=jnp.float32)
    return gram + reg_weight * bin_power / SPEAKERS * direction


def solution(mesh):
    placed = (
        P(("band", "spk"), None, None),
        P(("band", "spk"), None, None, None),
        P(("band", "spk"), None),
        P("band", "spk", None),
    )
    return jax.shard_map(
        per_device,
        mesh=mesh,
        in_specs=placed,
        out_specs=P(("band", "spk"), None, None),
        check_vma=False,
    )
```

```python
import jax
import jax.numpy as jnp
from jax import lax
from jax.sharding import PartitionSpec as P

SBLK = 32
MBLK = 128
SPEAKERS = 4096


reg_weight = 0.25


def swap_halves(rows, sign):
    width = rows.shape[-2]
    half = width // 2
    col = jnp.arange(width)
    flip = ((col[:, None] + half) % width == col[None, :]).astype(rows.dtype)
    flip = flip * jnp.where(col[None, :] < half, -sign, sign).astype(rows.dtype)
    return jnp.einsum("...ki,kl->...li", rows, flip, preferred_element_type=jnp.float32).astype(rows.dtype)


def slot_ranks(target_peer, devices):
    onehot = (target_peer[..., :, None] == jnp.arange(devices)).astype(jnp.int32)
    running = jnp.cumsum(onehot, axis=-2)
    return jnp.take_along_axis(running, target_peer[..., None], axis=-1)[..., 0] - 1


def with_header(blocks, values, devices, capacity):
    rows, lanes = blocks.shape[1], blocks.shape[2]
    body = blocks.reshape(devices, capacity * rows, lanes)
    head = jnp.pad(values.astype(blocks.dtype)[:, None, :], ((0, 0), (0, 15), (0, lanes - values.shape[1])))
    return jnp.concatenate([body, head], axis=1)


def split_header(buffer, capacity, rows, width):
    body = buffer[:, : capacity * rows].reshape(-1, rows, buffer.shape[2])
    return body, buffer[:, capacity * rows, :width]


def per_device(direction, plant, tile_pairs, mic_weight):
    devices = lax.axis_size("spk")
    device_id = lax.axis_index("spk")
    unit_count = direction.shape[0]
    tile_count = plant.shape[0]
    block_size = direction.shape[1]
    field_width = direction.shape[2]
    groups_per_bin = SBLK // unit_count
    bin_count = devices // groups_per_bin
    peer_blocks = MBLK // devices
    mic_units = bin_count * peer_blocks
    my_bin = device_id // groups_per_bin
    capacity = max(3, (2 * tile_count + devices - 1) // devices)
    slots = devices * capacity

    local_unit = tile_pairs[:, 0] % unit_count
    mic_block = tile_pairs[:, 1]
    target_peer = mic_block // peer_blocks
    position = target_peer * capacity + slot_ranks(target_peer, devices)
    send_hit = position[None, :] == jnp.arange(slots)[:, None]
    slot_pair = jnp.sum(jnp.where(send_hit, jnp.arange(tile_count), 0), axis=1)
    target_label = my_bin * peer_blocks + mic_block - target_peer * peer_blocks
    slot_label = jnp.where(
        send_hit.any(axis=1), jnp.sum(jnp.where(send_hit, target_label, 0), axis=1), mic_units
    )

    rounded = jnp.swapaxes(direction.astype(jnp.bfloat16), 1, 2)
    both = jnp.stack([rounded, swap_halves(rounded, 1)], axis=1)
    pair_rows = both[local_unit]
    partial_field = jnp.einsum("tcij,tckj->tki", plant, pair_rows,
                               preferred_element_type=jnp.float32).astype(jnp.bfloat16)
    outgoing = jnp.take(partial_field, slot_pair, axis=0, mode="clip")
    squares = jnp.square(plant.astype(jnp.float32)).reshape(-1, 8, block_size)
    local_power = jnp.sum(lax.optimization_barrier(jnp.sum(squares, axis=0)))
    power_hi = local_power.astype(jnp.bfloat16).astype(jnp.float32)
    power_mid = (local_power - power_hi).astype(jnp.bfloat16).astype(jnp.float32)
    power_lo = local_power - power_hi - power_mid
    power_parts = jnp.broadcast_to(jnp.stack([power_hi, power_mid, power_lo]), (devices, 3))
    header = jnp.concatenate([slot_label.reshape(devices, capacity).astype(jnp.float32), power_parts], axis=1)
    sent = with_header(outgoing, header, devices, capacity)
    arrived, header_in = split_header(
        lax.all_to_all(sent, "spk", 0, 0, tiled=True), capacity, field_width, capacity + 3)
    labels_in = header_in[:, :capacity].astype(jnp.int32).reshape(slots)
    source_bin = jnp.arange(devices) // groups_per_bin
    power_of = jnp.sum(header_in[:, capacity:].astype(jnp.float32), axis=1)
    bin_power = jnp.sum(jnp.where(source_bin == my_bin, power_of, 0.0))
    recv_onehot = (labels_in[None, :] == jnp.arange(mic_units)[:, None]).astype(jnp.bfloat16)
    pressure = jnp.einsum("ms,ski->mki", recv_onehot, arrived, preferred_element_type=jnp.float32)
    weights_flat = mic_weight.reshape(mic_units, block_size)
    weighted = (weights_flat[:, None, :] * pressure).astype(jnp.bfloat16)

    reply = jnp.take(weighted, jnp.minimum(labels_in, mic_units - 1), axis=0, mode="clip")
    returned = lax.all_to_all(
        reply.reshape(devices, capacity * field_width, block_size), "spk", 0, 0, tiled=True
    ).reshape(slots, field_width, block_size)
    tile_weighted = jnp.take(returned, position, axis=0, mode="clip")

    back_rows = jnp.stack([tile_weighted, swap_halves(tile_weighted, -1)], axis=1)
    unit_mask = (local_unit[:, None] == jnp.arange(unit_count)[None, :]).astype(jnp.bfloat16)
    masked = back_rows[:, None] * unit_mask[:, :, None, None, None]
    gram = jnp.einsum("tcij,tucki->ujk", plant, masked, preferred_element_type=jnp.float32)
    return gram + reg_weight * bin_power / SPEAKERS * direction


def solution(mesh):
    placed = (
        P(("band", "spk"), None, None),
        P(("band", "spk"), None, None, None),
        P(("band", "spk"), None),
        P("band", "spk", None),
    )
    return jax.shard_map(
        per_device,
        mesh=mesh,
        in_specs=placed,
        out_specs=P(("band", "spk"), None, None),
        check_vma=False,
    )
```

```python
import jax
import jax.numpy as jnp
from jax import lax
from jax.sharding import PartitionSpec as P

SBLK = 32
MBLK = 128
SPEAKERS = 4096


reg_weight = 0.25


def swap_halves(rows, sign):
    width = rows.shape[-2]
    half = width // 2
    col = jnp.arange(width)
    flip = ((col[:, None] + half) % width == col[None, :]).astype(rows.dtype)
    flip = flip * jnp.where(col[None, :] < half, -sign, sign).astype(rows.dtype)
    return jnp.einsum("...ki,kl->...li", rows, flip, preferred_element_type=jnp.float32).astype(rows.dtype)


def slot_ranks(target_peer, devices):
    count = target_peer.shape[-1]
    earlier = jnp.arange(count)[None, :] < jnp.arange(count)[:, None]
    same = target_peer[:, None] == target_peer[None, :]
    return jnp.sum((earlier & same).astype(jnp.int32), axis=1)


def with_header(blocks, values, devices, capacity):
    rows, lanes = blocks.shape[1], blocks.shape[2]
    body = blocks.reshape(devices, capacity * rows, lanes)
    head = jnp.pad(values.astype(blocks.dtype)[:, None, :], ((0, 0), (0, 15), (0, lanes - values.shape[1])))
    return jnp.concatenate([body, head], axis=1)


def split_header(buffer, capacity, rows, width):
    body = buffer[:, : capacity * rows].reshape(-1, rows, buffer.shape[2])
    return body, buffer[:, capacity * rows, :width]


def per_device(direction, plant, tile_pairs, mic_weight):
    devices = lax.axis_size("spk")
    device_id = lax.axis_index("spk")
    unit_count = direction.shape[0]
    tile_count = plant.shape[0]
    block_size = direction.shape[1]
    field_width = direction.shape[2]
    groups_per_bin = SBLK // unit_count
    bin_count = devices // groups_per_bin
    peer_blocks = MBLK // devices
    mic_units = bin_count * peer_blocks
    my_bin = device_id // groups_per_bin
    capacity = max(3, (2 * tile_count + devices - 1) // devices)
    slots = devices * capacity

    local_unit = tile_pairs[:, 0] % unit_count
    mic_block = tile_pairs[:, 1]
    target_peer = mic_block // peer_blocks
    position = target_peer * capacity + slot_ranks(target_peer, devices)
    send_hit = position[None, :] == jnp.arange(slots)[:, None]
    slot_pair = jnp.sum(jnp.where(send_hit, jnp.arange(tile_count), 0), axis=1)
    target_label = my_bin * peer_blocks + mic_block - target_peer * peer_blocks
    slot_label = jnp.where(
        send_hit.any(axis=1), jnp.sum(jnp.where(send_hit, target_label, 0), axis=1), mic_units
    )

    rounded = jnp.swapaxes(direction.astype(jnp.bfloat16), 1, 2)
    both = jnp.stack([rounded, swap_halves(rounded, 1)], axis=1)
    pair_rows = both[local_unit]
    partial_field = jnp.einsum("tcij,tckj->tki", plant, pair_rows,
                               preferred_element_type=jnp.float32).astype(jnp.bfloat16)
    outgoing = jnp.take(partial_field, slot_pair, axis=0, mode="clip")
    local_power = jnp.trace(jnp.einsum("tcij,tcik->jk", plant, plant,
                                       preferred_element_type=jnp.float32))
    power_hi = local_power.astype(jnp.bfloat16).astype(jnp.float32)
    power_mid = (local_power - power_hi).astype(jnp.bfloat16).astype(jnp.float32)
    power_lo = local_power - power_hi - power_mid
    power_parts = jnp.broadcast_to(jnp.stack([power_hi, power_mid, power_lo]), (devices, 3))
    header = jnp.concatenate([slot_label.reshape(devices, capacity).astype(jnp.float32), power_parts], axis=1)
    sent = with_header(outgoing, header, devices, capacity)
    arrived, header_in = split_header(
        lax.all_to_all(sent, "spk", 0, 0, tiled=True), capacity, field_width, capacity + 3)
    labels_in = header_in[:, :capacity].astype(jnp.int32).reshape(slots)
    source_bin = jnp.arange(devices) // groups_per_bin
    power_of = jnp.sum(header_in[:, capacity:].astype(jnp.float32), axis=1)
    bin_power = jnp.sum(jnp.where(source_bin == my_bin, power_of, 0.0))
    recv_onehot = (labels_in[None, :] == jnp.arange(mic_units)[:, None]).astype(jnp.bfloat16)
    pressure = jnp.einsum("ms,ski->mki", recv_onehot, arrived, preferred_element_type=jnp.float32)
    weights_flat = mic_weight.reshape(mic_units, block_size)
    weighted = (weights_flat[:, None, :] * pressure).astype(jnp.bfloat16)

    reply = jnp.take(weighted, jnp.minimum(labels_in, mic_units - 1), axis=0, mode="clip")
    returned = lax.all_to_all(
        reply.reshape(devices, capacity * field_width, block_size), "spk", 0, 0, tiled=True
    ).reshape(slots, field_width, block_size)
    tile_weighted = jnp.take(returned, position, axis=0, mode="clip")

    back_rows = jnp.stack([tile_weighted, swap_halves(tile_weighted, -1)], axis=1)
    unit_mask = (local_unit[:, None] == jnp.arange(unit_count)[None, :]).astype(jnp.bfloat16)
    masked = back_rows[:, None] * unit_mask[:, :, None, None, None]
    gram = jnp.einsum("tcij,tucki->ujk", plant, masked, preferred_element_type=jnp.float32)
    return gram + reg_weight * bin_power / SPEAKERS * direction


def solution(mesh):
    placed = (
        P(("band", "spk"), None, None),
        P(("band", "spk"), None, None, None),
        P(("band", "spk"), None),
        P("band", "spk", None),
    )
    return jax.shard_map(
        per_device,
        mesh=mesh,
        in_specs=placed,
        out_specs=P(("band", "spk"), None, None),
        check_vma=False,
    )
```

```python
import jax
import jax.numpy as jnp
from jax import lax
from jax.sharding import PartitionSpec as P
from jax.experimental import pallas as pl
from jax.experimental.pallas import tpu as pltpu

SBLK = 32
MBLK = 128
SPEAKERS = 4096


reg_weight = 0.25


def swap_halves(rows, sign):
    width = rows.shape[-2]
    half = width // 2
    col = jnp.arange(width)
    flip = ((col[:, None] + half) % width == col[None, :]).astype(rows.dtype)
    flip = flip * jnp.where(col[None, :] < half, -sign, sign).astype(rows.dtype)
    return jnp.einsum("...ki,kl->...li", rows, flip, preferred_element_type=jnp.float32).astype(rows.dtype)


def _forward_kernel(unit_ref, plant_ref, rows_ref, out_ref, power_ref):
    pair = pl.program_id(0)
    dims = (((1,), (1,)), ((), ()))
    acc = lax.dot_general(rows_ref[0, 0], plant_ref[0, 0], dims, preferred_element_type=jnp.float32)
    acc = acc + lax.dot_general(rows_ref[0, 1], plant_ref[0, 1], dims, preferred_element_type=jnp.float32)
    out_ref[0] = acc.astype(out_ref.dtype)

    @pl.when(pair == 0)
    def _():
        power_ref[...] = jnp.zeros_like(power_ref)

    wide = plant_ref[0].astype(jnp.float32)
    sq = wide * wide
    power_ref[...] += jnp.sum(sq.reshape(-1, 8, sq.shape[-1]), axis=0)

def forward_and_power(plant, rows, unit, interpret=False):
    tiles, _, block, width = plant.shape
    fw = rows.shape[2]
    grid_spec = pltpu.PrefetchScalarGridSpec(
        num_scalar_prefetch=1,
        grid=(tiles,),
        in_specs=[
            pl.BlockSpec((1, 2, block, width), lambda t, u: (t, 0, 0, 0)),
            pl.BlockSpec((1, 2, fw, width), lambda t, u: (u[t], 0, 0, 0)),
        ],
        out_specs=[
            pl.BlockSpec((1, fw, block), lambda t, u: (t, 0, 0)),
            pl.BlockSpec((8, width), lambda t, u: (0, 0)),
        ],
    )
    return pl.pallas_call(
        _forward_kernel,
        grid_spec=grid_spec,
        out_shape=[jax.ShapeDtypeStruct((tiles, fw, block), jnp.bfloat16),
                   jax.ShapeDtypeStruct((8, width), jnp.float32)],
        interpret=interpret,
    )(unit, plant, rows)

def slot_ranks(target_peer, devices):
    count = target_peer.shape[-1]
    earlier = jnp.arange(count)[None, :] < jnp.arange(count)[:, None]
    same = target_peer[:, None] == target_peer[None, :]
    return jnp.sum((earlier & same).astype(jnp.int32), axis=1)


def with_header(blocks, values, devices, capacity):
    rows, lanes = blocks.shape[1], blocks.shape[2]
    body = blocks.reshape(devices, capacity * rows, lanes)
    head = jnp.pad(values.astype(blocks.dtype)[:, None, :], ((0, 0), (0, 15), (0, lanes - values.shape[1])))
    return jnp.concatenate([body, head], axis=1)


def split_header(buffer, capacity, rows, width):
    body = buffer[:, : capacity * rows].reshape(-1, rows, buffer.shape[2])
    return body, buffer[:, capacity * rows, :width]


def per_device(direction, plant, tile_pairs, mic_weight):
    devices = lax.axis_size("spk")
    device_id = lax.axis_index("spk")
    unit_count = direction.shape[0]
    tile_count = plant.shape[0]
    block_size = direction.shape[1]
    field_width = direction.shape[2]
    groups_per_bin = SBLK // unit_count
    bin_count = devices // groups_per_bin
    peer_blocks = MBLK // devices
    mic_units = bin_count * peer_blocks
    my_bin = device_id // groups_per_bin
    capacity = max(3, (2 * tile_count + devices - 1) // devices)
    slots = devices * capacity

    local_unit = tile_pairs[:, 0] % unit_count
    mic_block = tile_pairs[:, 1]
    target_peer = mic_block // peer_blocks
    position = target_peer * capacity + slot_ranks(target_peer, devices)
    send_hit = position[None, :] == jnp.arange(slots)[:, None]
    slot_pair = jnp.sum(jnp.where(send_hit, jnp.arange(tile_count), 0), axis=1)
    target_label = my_bin * peer_blocks + mic_block - target_peer * peer_blocks
    slot_label = jnp.where(
        send_hit.any(axis=1), jnp.sum(jnp.where(send_hit, target_label, 0), axis=1), mic_units
    )

    rounded = jnp.swapaxes(direction.astype(jnp.bfloat16), 1, 2)
    both = jnp.stack([rounded, swap_halves(rounded, 1)], axis=1)
    partial_field, power_tile = forward_and_power(plant, both, local_unit)
    outgoing = jnp.take(partial_field, slot_pair, axis=0, mode="clip")
    local_power = jnp.sum(power_tile)
    power_hi = local_power.astype(jnp.bfloat16).astype(jnp.float32)
    power_mid = (local_power - power_hi).astype(jnp.bfloat16).astype(jnp.float32)
    power_lo = local_power - power_hi - power_mid
    power_parts = jnp.broadcast_to(jnp.stack([power_hi, power_mid, power_lo]), (devices, 3))
    header = jnp.concatenate([slot_label.reshape(devices, capacity).astype(jnp.float32), power_parts], axis=1)
    sent = with_header(outgoing, header, devices, capacity)
    arrived, header_in = split_header(
        lax.all_to_all(sent, "spk", 0, 0, tiled=True), capacity, field_width, capacity + 3)
    labels_in = header_in[:, :capacity].astype(jnp.int32).reshape(slots)
    source_bin = jnp.arange(devices) // groups_per_bin
    power_of = jnp.sum(header_in[:, capacity:].astype(jnp.float32), axis=1)
    bin_power = jnp.sum(jnp.where(source_bin == my_bin, power_of, 0.0))
    recv_onehot = (labels_in[None, :] == jnp.arange(mic_units)[:, None]).astype(jnp.bfloat16)
    pressure = jnp.einsum("ms,ski->mki", recv_onehot, arrived, preferred_element_type=jnp.float32)
    weights_flat = mic_weight.reshape(mic_units, block_size)
    weighted = (weights_flat[:, None, :] * pressure).astype(jnp.bfloat16)

    reply = jnp.take(weighted, jnp.minimum(labels_in, mic_units - 1), axis=0, mode="clip")
    returned = lax.all_to_all(
        reply.reshape(devices, capacity * field_width, block_size), "spk", 0, 0, tiled=True
    ).reshape(slots, field_width, block_size)
    tile_weighted = jnp.take(returned, position, axis=0, mode="clip")

    back_rows = jnp.stack([tile_weighted, swap_halves(tile_weighted, -1)], axis=1)
    unit_mask = (local_unit[:, None] == jnp.arange(unit_count)[None, :]).astype(jnp.bfloat16)
    masked = back_rows[:, None] * unit_mask[:, :, None, None, None]
    gram = jnp.einsum("tcij,tucki->ujk", plant, masked, preferred_element_type=jnp.float32)
    return gram + reg_weight * bin_power / SPEAKERS * direction


def solution(mesh):
    placed = (
        P(("band", "spk"), None, None),
        P(("band", "spk"), None, None, None),
        P(("band", "spk"), None),
        P("band", "spk", None),
    )
    return jax.shard_map(
        per_device,
        mesh=mesh,
        in_specs=placed,
        out_specs=P(("band", "spk"), None, None),
        check_vma=False,
    )
```

```python
import jax
import jax.numpy as jnp
from jax import lax
from jax.sharding import PartitionSpec as P
from jax.experimental import pallas as pl
from jax.experimental.pallas import tpu as pltpu

SBLK = 32
MBLK = 128
SPEAKERS = 4096


reg_weight = 0.25


def swap_halves(rows, sign):
    width = rows.shape[-2]
    half = width // 2
    col = jnp.arange(width)
    flip = ((col[:, None] + half) % width == col[None, :]).astype(rows.dtype)
    flip = flip * jnp.where(col[None, :] < half, -sign, sign).astype(rows.dtype)
    return jnp.einsum("...ki,kl->...li", rows, flip, preferred_element_type=jnp.float32).astype(rows.dtype)


def _forward_kernel(unit_ref, plant_ref, rows_ref, out_ref, power_ref):
    dims = (((1,), (1,)), ((), ()))
    lanes = plant_ref.shape[-1]

    def body(pair, power):
        unit = unit_ref[pair]
        acc = lax.dot_general(rows_ref[unit, 0], plant_ref[pair, 0], dims, preferred_element_type=jnp.float32)
        acc = acc + lax.dot_general(rows_ref[unit, 1], plant_ref[pair, 1], dims, preferred_element_type=jnp.float32)
        out_ref[pair] = acc.astype(out_ref.dtype)
        wide = plant_ref[pair].astype(jnp.float32)
        return power + jnp.sum((wide * wide).reshape(-1, 8, lanes), axis=0)

    power_ref[...] = lax.fori_loop(0, plant_ref.shape[0], body, jnp.zeros((8, lanes), jnp.float32))

def forward_and_power(plant, rows, unit, interpret=False):
    tiles, _, block, width = plant.shape
    fw = rows.shape[2]
    grid_spec = pltpu.PrefetchScalarGridSpec(
        num_scalar_prefetch=1,
        grid=(1,),
        in_specs=[
            pl.BlockSpec(plant.shape, lambda i, u: (0, 0, 0, 0)),
            pl.BlockSpec(rows.shape, lambda i, u: (0, 0, 0, 0)),
        ],
        out_specs=[
            pl.BlockSpec((tiles, fw, block), lambda i, u: (0, 0, 0)),
            pl.BlockSpec((8, width), lambda i, u: (0, 0)),
        ],
    )
    return pl.pallas_call(
        _forward_kernel,
        grid_spec=grid_spec,
        out_shape=[jax.ShapeDtypeStruct((tiles, fw, block), jnp.bfloat16),
                   jax.ShapeDtypeStruct((8, width), jnp.float32)],
        interpret=interpret,
    )(unit, plant, rows)

def slot_ranks(target_peer, devices):
    count = target_peer.shape[-1]
    earlier = jnp.arange(count)[None, :] < jnp.arange(count)[:, None]
    same = target_peer[:, None] == target_peer[None, :]
    return jnp.sum((earlier & same).astype(jnp.int32), axis=1)


def with_header(blocks, values, devices, capacity):
    rows, lanes = blocks.shape[1], blocks.shape[2]
    body = blocks.reshape(devices, capacity * rows, lanes)
    head = jnp.pad(values.astype(blocks.dtype)[:, None, :], ((0, 0), (0, 15), (0, lanes - values.shape[1])))
    return jnp.concatenate([body, head], axis=1)


def split_header(buffer, capacity, rows, width):
    body = buffer[:, : capacity * rows].reshape(-1, rows, buffer.shape[2])
    return body, buffer[:, capacity * rows, :width]


def per_device(direction, plant, tile_pairs, mic_weight):
    devices = lax.axis_size("spk")
    device_id = lax.axis_index("spk")
    unit_count = direction.shape[0]
    tile_count = plant.shape[0]
    block_size = direction.shape[1]
    field_width = direction.shape[2]
    groups_per_bin = SBLK // unit_count
    bin_count = devices // groups_per_bin
    peer_blocks = MBLK // devices
    mic_units = bin_count * peer_blocks
    my_bin = device_id // groups_per_bin
    capacity = max(3, (2 * tile_count + devices - 1) // devices)
    slots = devices * capacity

    local_unit = tile_pairs[:, 0] % unit_count
    mic_block = tile_pairs[:, 1]
    target_peer = mic_block // peer_blocks
    position = target_peer * capacity + slot_ranks(target_peer, devices)
    send_hit = position[None, :] == jnp.arange(slots)[:, None]
    slot_pair = jnp.sum(jnp.where(send_hit, jnp.arange(tile_count), 0), axis=1)
    target_label = my_bin * peer_blocks + mic_block - target_peer * peer_blocks
    slot_label = jnp.where(
        send_hit.any(axis=1), jnp.sum(jnp.where(send_hit, target_label, 0), axis=1), mic_units
    )

    rounded = jnp.swapaxes(direction.astype(jnp.bfloat16), 1, 2)
    both = jnp.stack([rounded, swap_halves(rounded, 1)], axis=1)
    partial_field, power_tile = forward_and_power(plant, both, local_unit)
    outgoing = jnp.take(partial_field, slot_pair, axis=0, mode="clip")
    local_power = jnp.sum(power_tile)
    power_hi = local_power.astype(jnp.bfloat16).astype(jnp.float32)
    power_mid = (local_power - power_hi).astype(jnp.bfloat16).astype(jnp.float32)
    power_lo = local_power - power_hi - power_mid
    power_parts = jnp.broadcast_to(jnp.stack([power_hi, power_mid, power_lo]), (devices, 3))
    header = jnp.concatenate([slot_label.reshape(devices, capacity).astype(jnp.float32), power_parts], axis=1)
    sent = with_header(outgoing, header, devices, capacity)
    arrived, header_in = split_header(
        lax.all_to_all(sent, "spk", 0, 0, tiled=True), capacity, field_width, capacity + 3)
    labels_in = header_in[:, :capacity].astype(jnp.int32).reshape(slots)
    source_bin = jnp.arange(devices) // groups_per_bin
    power_of = jnp.sum(header_in[:, capacity:].astype(jnp.float32), axis=1)
    bin_power = jnp.sum(jnp.where(source_bin == my_bin, power_of, 0.0))
    recv_onehot = (labels_in[None, :] == jnp.arange(mic_units)[:, None]).astype(jnp.bfloat16)
    pressure = jnp.einsum("ms,ski->mki", recv_onehot, arrived, preferred_element_type=jnp.float32)
    weights_flat = mic_weight.reshape(mic_units, block_size)
    weighted = (weights_flat[:, None, :] * pressure).astype(jnp.bfloat16)

    reply = jnp.take(weighted, jnp.minimum(labels_in, mic_units - 1), axis=0, mode="clip")
    returned = lax.all_to_all(
        reply.reshape(devices, capacity * field_width, block_size), "spk", 0, 0, tiled=True
    ).reshape(slots, field_width, block_size)
    tile_weighted = jnp.take(returned, position, axis=0, mode="clip")

    back_rows = jnp.stack([tile_weighted, swap_halves(tile_weighted, -1)], axis=1)
    unit_mask = (local_unit[:, None] == jnp.arange(unit_count)[None, :]).astype(jnp.bfloat16)
    masked = back_rows[:, None] * unit_mask[:, :, None, None, None]
    gram = jnp.einsum("tcij,tucki->ujk", plant, masked, preferred_element_type=jnp.float32)
    return gram + reg_weight * bin_power / SPEAKERS * direction


def solution(mesh):
    placed = (
        P(("band", "spk"), None, None),
        P(("band", "spk"), None, None, None),
        P(("band", "spk"), None),
        P("band", "spk", None),
    )
    return jax.shard_map(
        per_device,
        mesh=mesh,
        in_specs=placed,
        out_specs=P(("band", "spk"), None, None),
        check_vma=False,
    )
```

```python
import jax
import jax.numpy as jnp
from jax import lax
from jax.sharding import PartitionSpec as P

SBLK = 32
MBLK = 128
SPEAKERS = 4096


reg_weight = 0.25


def swap_halves(rows, sign):
    width = rows.shape[-2]
    half = width // 2
    col = jnp.arange(width)
    flip = ((col[:, None] + half) % width == col[None, :]).astype(rows.dtype)
    flip = flip * jnp.where(col[None, :] < half, -sign, sign).astype(rows.dtype)
    return jnp.einsum("...ki,kl->...li", rows, flip, preferred_element_type=jnp.float32).astype(rows.dtype)


def slot_ranks(target_peer, devices):
    count = target_peer.shape[-1]
    earlier = jnp.arange(count)[None, :] < jnp.arange(count)[:, None]
    same = target_peer[:, None] == target_peer[None, :]
    return jnp.sum((earlier & same).astype(jnp.int32), axis=1)


def with_header(blocks, values, devices, capacity):
    rows, lanes = blocks.shape[1], blocks.shape[2]
    body = blocks.reshape(devices, capacity * rows, lanes)
    head = jnp.pad(values.astype(blocks.dtype)[:, None, :], ((0, 0), (0, 15), (0, lanes - values.shape[1])))
    return jnp.concatenate([body, head], axis=1)


def split_header(buffer, capacity, rows, width):
    body = buffer[:, : capacity * rows].reshape(-1, rows, buffer.shape[2])
    return body, buffer[:, capacity * rows, :width]


def per_device(direction, plant, tile_pairs, mic_weight):
    devices = lax.axis_size("spk")
    device_id = lax.axis_index("spk")
    unit_count = direction.shape[0]
    tile_count = plant.shape[0]
    block_size = direction.shape[1]
    field_width = direction.shape[2]
    groups_per_bin = SBLK // unit_count
    bin_count = devices // groups_per_bin
    peer_blocks = MBLK // devices
    mic_units = bin_count * peer_blocks
    my_bin = device_id // groups_per_bin
    capacity = max(3, (2 * tile_count + devices - 1) // devices)
    slots = devices * capacity

    local_unit = tile_pairs[:, 0] % unit_count
    mic_block = tile_pairs[:, 1]
    target_peer = mic_block // peer_blocks
    position = target_peer * capacity + slot_ranks(target_peer, devices)
    send_hit = position[None, :] == jnp.arange(slots)[:, None]
    slot_pair = jnp.sum(jnp.where(send_hit, jnp.arange(tile_count), 0), axis=1)
    target_label = my_bin * peer_blocks + mic_block - target_peer * peer_blocks
    slot_label = jnp.where(
        send_hit.any(axis=1), jnp.sum(jnp.where(send_hit, target_label, 0), axis=1), mic_units
    )

    rounded = jnp.swapaxes(direction.astype(jnp.bfloat16), 1, 2)
    both = jnp.stack([rounded, swap_halves(rounded, 1)], axis=1)
    pair_rows = both[local_unit]
    partial_field = jnp.einsum("tcij,tckj->tki", plant, pair_rows,
                               preferred_element_type=jnp.float32).astype(jnp.bfloat16)
    outgoing = jnp.take(partial_field, slot_pair, axis=0, mode="clip")
    sent = with_header(outgoing, slot_label.reshape(devices, capacity), devices, capacity)
    arrived, header_in = split_header(
        lax.all_to_all(sent, "spk", 0, 0, tiled=True), capacity, field_width, capacity)
    labels_in = header_in.astype(jnp.int32).reshape(slots)
    recv_onehot = (labels_in[None, :] == jnp.arange(mic_units)[:, None]).astype(jnp.bfloat16)
    pressure = jnp.einsum("ms,ski->mki", recv_onehot, arrived, preferred_element_type=jnp.float32)
    weights_flat = mic_weight.reshape(mic_units, block_size)
    weighted = (weights_flat[:, None, :] * pressure).astype(jnp.bfloat16)

    local_power = jnp.trace(jnp.einsum("tcij,tcik->jk", plant, plant,
                                       preferred_element_type=jnp.float32))
    power_hi = local_power.astype(jnp.bfloat16).astype(jnp.float32)
    power_mid = (local_power - power_hi).astype(jnp.bfloat16).astype(jnp.float32)
    power_lo = local_power - power_hi - power_mid
    power_row = jnp.zeros((16, block_size), jnp.float32).at[0, :3].set(
        jnp.stack([power_hi, power_mid, power_lo])).astype(jnp.bfloat16)
    groups = field_width // 16
    per_peer = capacity * groups + 1
    source_rows = jnp.concatenate(
        [weighted.reshape(mic_units * groups, 16, block_size), power_row[None]], axis=0)
    reply_group = (jnp.minimum(labels_in, mic_units - 1) * groups)[:, None] + jnp.arange(groups)
    reply_index = jnp.concatenate(
        [reply_group.reshape(devices, capacity * groups),
         jnp.full((devices, 1), mic_units * groups, jnp.int32)], axis=1)
    reply = jnp.take(source_rows, reply_index.reshape(-1), axis=0, mode="clip")
    returned = lax.all_to_all(
        reply.reshape(devices, per_peer * 16, block_size), "spk", 0, 0, tiled=True)
    source_bin = jnp.arange(devices) // groups_per_bin
    power_of = jnp.sum(returned[:, capacity * field_width, :3].astype(jnp.float32), axis=1)
    bin_power = jnp.sum(jnp.where(source_bin == my_bin, power_of, 0.0))
    rank = position - target_peer * capacity
    pick = (target_peer * per_peer + rank * groups)[:, None] + jnp.arange(groups)
    tile_weighted = jnp.take(returned.reshape(devices * per_peer, 16, block_size), pick.reshape(-1),
                             axis=0, mode="clip").reshape(tile_count, field_width, block_size)

    back_rows = jnp.stack([tile_weighted, swap_halves(tile_weighted, -1)], axis=1)
    unit_mask = (local_unit[:, None] == jnp.arange(unit_count)[None, :]).astype(jnp.bfloat16)
    masked = back_rows[:, None] * unit_mask[:, :, None, None, None]
    gram = jnp.einsum("tcij,tucki->ujk", plant, masked, preferred_element_type=jnp.float32)
    return gram + reg_weight * bin_power / SPEAKERS * direction


def solution(mesh):
    placed = (
        P(("band", "spk"), None, None),
        P(("band", "spk"), None, None, None),
        P(("band", "spk"), None),
        P("band", "spk", None),
    )
    return jax.shard_map(
        per_device,
        mesh=mesh,
        in_specs=placed,
        out_specs=P(("band", "spk"), None, None),
        check_vma=False,
    )
```

```python
import jax
import jax.numpy as jnp
from jax import lax
from jax.sharding import PartitionSpec as P

SBLK = 32
MBLK = 128
SPEAKERS = 4096


reg_weight = 0.25


def swap_halves(rows, sign):
    width = rows.shape[-2]
    half = width // 2
    col = jnp.arange(width)
    flip = ((col[:, None] + half) % width == col[None, :]).astype(rows.dtype)
    flip = flip * jnp.where(col[None, :] < half, -sign, sign).astype(rows.dtype)
    return jnp.einsum("...ki,kl->...li", rows, flip, preferred_element_type=jnp.float32).astype(rows.dtype)


def slot_ranks(target_peer, devices):
    count = target_peer.shape[-1]
    earlier = jnp.arange(count)[None, :] < jnp.arange(count)[:, None]
    same = target_peer[:, None] == target_peer[None, :]
    return jnp.sum((earlier & same).astype(jnp.int32), axis=1)


def with_header(blocks, values, devices, capacity):
    rows, lanes = blocks.shape[1], blocks.shape[2]
    body = blocks.reshape(devices, capacity * rows, lanes)
    head = jnp.pad(values.astype(blocks.dtype)[:, None, :], ((0, 0), (0, 15), (0, lanes - values.shape[1])))
    return jnp.concatenate([body, head], axis=1)


def split_header(buffer, capacity, rows, width):
    body = buffer[:, : capacity * rows].reshape(-1, rows, buffer.shape[2])
    return body, buffer[:, capacity * rows, :width]


def exchange(blocks, devices, direction):
    received = [blocks[0]]
    for shift in range(1, devices):
        pairs = [(i, (i + direction * shift) % devices) for i in range(devices)]
        received.append(lax.ppermute(blocks[shift], "spk", pairs))
    return jnp.stack(received)


def per_device(direction, plant, tile_pairs, mic_weight):
    devices = lax.axis_size("spk")
    device_id = lax.axis_index("spk")
    unit_count = direction.shape[0]
    tile_count = plant.shape[0]
    block_size = direction.shape[1]
    field_width = direction.shape[2]
    groups_per_bin = SBLK // unit_count
    bin_count = devices // groups_per_bin
    peer_blocks = MBLK // devices
    mic_units = bin_count * peer_blocks
    my_bin = device_id // groups_per_bin
    capacity = max(3, (2 * tile_count + devices - 1) // devices)
    slots = devices * capacity

    local_unit = tile_pairs[:, 0] % unit_count
    mic_block = tile_pairs[:, 1]
    target_peer = mic_block // peer_blocks
    shift_of = (target_peer - device_id) % devices
    position = shift_of * capacity + slot_ranks(target_peer, devices)
    send_hit = position[None, :] == jnp.arange(slots)[:, None]
    slot_pair = jnp.sum(jnp.where(send_hit, jnp.arange(tile_count), 0), axis=1)
    target_label = my_bin * peer_blocks + mic_block - target_peer * peer_blocks
    slot_label = jnp.where(
        send_hit.any(axis=1), jnp.sum(jnp.where(send_hit, target_label, 0), axis=1), mic_units
    )

    rounded = jnp.swapaxes(direction.astype(jnp.bfloat16), 1, 2)
    both = jnp.stack([rounded, swap_halves(rounded, 1)], axis=1)
    pair_rows = both[local_unit]
    partial_field = jnp.einsum("tcij,tckj->tki", plant, pair_rows,
                               preferred_element_type=jnp.float32).astype(jnp.bfloat16)
    outgoing = jnp.take(partial_field, slot_pair, axis=0, mode="clip")
    local_power = jnp.trace(jnp.einsum("tcij,tcik->jk", plant, plant,
                                       preferred_element_type=jnp.float32))
    power_hi = local_power.astype(jnp.bfloat16).astype(jnp.float32)
    power_mid = (local_power - power_hi).astype(jnp.bfloat16).astype(jnp.float32)
    power_lo = local_power - power_hi - power_mid
    power_parts = jnp.broadcast_to(jnp.stack([power_hi, power_mid, power_lo]), (devices, 3))
    header = jnp.concatenate([slot_label.reshape(devices, capacity).astype(jnp.float32), power_parts], axis=1)
    sent = with_header(outgoing, header, devices, capacity)
    arrived, header_in = split_header(exchange(sent, devices, 1), capacity, field_width, capacity + 3)
    labels_in = header_in[:, :capacity].astype(jnp.int32).reshape(slots)
    source_bin = ((device_id - jnp.arange(devices)) % devices) // groups_per_bin
    power_of = jnp.sum(header_in[:, capacity:].astype(jnp.float32), axis=1)
    bin_power = jnp.sum(jnp.where(source_bin == my_bin, power_of, 0.0))
    recv_onehot = (labels_in[None, :] == jnp.arange(mic_units)[:, None]).astype(jnp.bfloat16)
    pressure = jnp.einsum("ms,ski->mki", recv_onehot, arrived, preferred_element_type=jnp.float32)
    weights_flat = mic_weight.reshape(mic_units, block_size)
    weighted = (weights_flat[:, None, :] * pressure).astype(jnp.bfloat16)

    reply = jnp.take(weighted, jnp.minimum(labels_in, mic_units - 1), axis=0, mode="clip")
    returned = exchange(reply.reshape(devices, capacity * field_width, block_size), devices, -1
                        ).reshape(slots, field_width, block_size)
    tile_weighted = jnp.take(returned, position, axis=0, mode="clip")

    back_rows = jnp.stack([tile_weighted, swap_halves(tile_weighted, -1)], axis=1)
    unit_mask = (local_unit[:, None] == jnp.arange(unit_count)[None, :]).astype(jnp.bfloat16)
    masked = back_rows[:, None] * unit_mask[:, :, None, None, None]
    gram = jnp.einsum("tcij,tucki->ujk", plant, masked, preferred_element_type=jnp.float32)
    return gram + reg_weight * bin_power / SPEAKERS * direction


def solution(mesh):
    placed = (
        P(("band", "spk"), None, None),
        P(("band", "spk"), None, None, None),
        P(("band", "spk"), None),
        P("band", "spk", None),
    )
    return jax.shard_map(
        per_device,
        mesh=mesh,
        in_specs=placed,
        out_specs=P(("band", "spk"), None, None),
        check_vma=False,
    )
```

```python
import jax
import jax.numpy as jnp
from jax import lax
from jax.sharding import PartitionSpec as P


SBLK = 32
MBLK = 128
SPEAKERS = 4096


reg_weight = 0.25


def swap_halves(rows, sign):
    width = rows.shape[-2]
    half = width // 2
    col = jnp.arange(width)
    flip = ((col[:, None] + half) % width == col[None, :]).astype(rows.dtype)
    flip = flip * jnp.where(col[None, :] < half, -sign, sign).astype(rows.dtype)
    return jnp.einsum("...ki,kl->...li", rows, flip, preferred_element_type=jnp.float32).astype(rows.dtype)


def slot_ranks(target_peer, devices):
    count = target_peer.shape[-1]
    earlier = jnp.arange(count)[None, :] < jnp.arange(count)[:, None]
    same = target_peer[:, None] == target_peer[None, :]
    return jnp.sum((earlier & same).astype(jnp.int32), axis=1)


def with_header(blocks, values, devices, capacity):
    rows, lanes = blocks.shape[1], blocks.shape[2]
    body = blocks.reshape(devices, capacity * rows, lanes)
    head = jnp.pad(values.astype(blocks.dtype)[:, None, :], ((0, 0), (0, 15), (0, lanes - values.shape[1])))
    return jnp.concatenate([body, head], axis=1)


def split_header(buffer, capacity, rows, width):
    body = buffer[:, : capacity * rows].reshape(-1, rows, buffer.shape[2])
    return body, buffer[:, capacity * rows, :width]


def exchange(blocks, devices, direction):
    received = [blocks[0]]
    for shift in range(1, devices):
        pairs = [(i, (i + direction * shift) % devices) for i in range(devices)]
        received.append(lax.ppermute(blocks[shift], "spk", pairs))
    return jnp.stack(received)


def per_device(direction, plant, tile_pairs, mic_weight):
    devices = lax.axis_size("spk")
    device_id = lax.axis_index("spk")
    unit_count = direction.shape[0]
    tile_count = plant.shape[0]
    block_size = direction.shape[1]
    field_width = direction.shape[2]
    groups_per_bin = SBLK // unit_count
    bin_count = devices // groups_per_bin
    peer_blocks = MBLK // devices
    mic_units = bin_count * peer_blocks
    my_bin = device_id // groups_per_bin
    capacity = max(3, (2 * tile_count + devices - 1) // devices)
    slots = devices * capacity

    local_unit = tile_pairs[:, 0] % unit_count
    mic_block = tile_pairs[:, 1]
    target_peer = mic_block // peer_blocks
    shift_of = (target_peer - device_id) % devices
    position = shift_of * capacity + slot_ranks(target_peer, devices)
    send_hit = position[None, :] == jnp.arange(slots)[:, None]
    slot_pair = jnp.sum(jnp.where(send_hit, jnp.arange(tile_count), 0), axis=1)
    target_label = my_bin * peer_blocks + mic_block - target_peer * peer_blocks
    slot_label = jnp.where(
        send_hit.any(axis=1), jnp.sum(jnp.where(send_hit, target_label, 0), axis=1), mic_units
    )

    rounded = jnp.swapaxes(direction.astype(jnp.bfloat16), 1, 2)
    both = jnp.stack([rounded, swap_halves(rounded, 1)], axis=1)
    pair_rows = both[local_unit]
    partial_field = jnp.einsum("tcij,tckj->tki", plant, pair_rows,
                               preferred_element_type=jnp.float32).astype(jnp.bfloat16)
    outgoing = jnp.take(partial_field, slot_pair, axis=0, mode="clip")
    sent = with_header(outgoing, slot_label.reshape(devices, capacity), devices, capacity)
    arrived, header_in = split_header(exchange(sent, devices, 1), capacity, field_width, capacity)
    labels_in = header_in.astype(jnp.int32).reshape(slots)
    recv_onehot = (labels_in[None, :] == jnp.arange(mic_units)[:, None]).astype(jnp.bfloat16)
    pressure = jnp.einsum("ms,ski->mki", recv_onehot, arrived, preferred_element_type=jnp.float32)
    weights_flat = mic_weight.reshape(mic_units, block_size)
    weighted = (weights_flat[:, None, :] * pressure).astype(jnp.bfloat16)

    local_power = jnp.trace(jnp.einsum("tcij,tcik->jk", plant, plant,
                                       preferred_element_type=jnp.float32))
    power_hi = local_power.astype(jnp.bfloat16).astype(jnp.float32)
    power_mid = (local_power - power_hi).astype(jnp.bfloat16).astype(jnp.float32)
    power_lo = local_power - power_hi - power_mid
    power_row = jnp.zeros((16, block_size), jnp.float32).at[0, :3].set(
        jnp.stack([power_hi, power_mid, power_lo])).astype(jnp.bfloat16)
    groups = field_width // 16
    per_peer = capacity * groups + 1
    source_rows = jnp.concatenate(
        [weighted.reshape(mic_units * groups, 16, block_size), power_row[None]], axis=0)
    reply_group = (jnp.minimum(labels_in, mic_units - 1) * groups)[:, None] + jnp.arange(groups)
    reply_index = jnp.concatenate(
        [reply_group.reshape(devices, capacity * groups),
         jnp.full((devices, 1), mic_units * groups, jnp.int32)], axis=1)
    reply = jnp.take(source_rows, reply_index.reshape(-1), axis=0, mode="clip")
    returned = exchange(reply.reshape(devices, per_peer * 16, block_size), devices, -1)
    source_bin = ((device_id + jnp.arange(devices)) % devices) // groups_per_bin
    power_of = jnp.sum(returned[:, capacity * field_width, :3].astype(jnp.float32), axis=1)
    bin_power = jnp.sum(jnp.where(source_bin == my_bin, power_of, 0.0))
    pick = (position // capacity * per_peer + position % capacity * groups)[:, None] + jnp.arange(groups)
    tile_weighted = jnp.take(returned.reshape(devices * per_peer, 16, block_size), pick.reshape(-1),
                             axis=0, mode="clip").reshape(tile_count, field_width, block_size)

    back_rows = jnp.stack([tile_weighted, swap_halves(tile_weighted, -1)], axis=1)
    unit_mask = (local_unit[:, None] == jnp.arange(unit_count)[None, :]).astype(jnp.bfloat16)
    masked = back_rows[:, None] * unit_mask[:, :, None, None, None]
    gram = jnp.einsum("tcij,tucki->ujk", plant, masked, preferred_element_type=jnp.float32)
    return gram + reg_weight * bin_power / SPEAKERS * direction


def solution(mesh):
    placed = (
        P(("band", "spk"), None, None),
        P(("band", "spk"), None, None, None),
        P(("band", "spk"), None),
        P("band", "spk", None),
    )
    return jax.shard_map(
        per_device,
        mesh=mesh,
        in_specs=placed,
        out_specs=P(("band", "spk"), None, None),
        check_vma=False,
    )
```

```python
import jax
import jax.numpy as jnp
from jax import lax
from jax.sharding import PartitionSpec as P


SBLK = 32
MBLK = 128
SPEAKERS = 4096


reg_weight = 0.25


def swap_halves(rows, sign):
    width = rows.shape[-2]
    half = width // 2
    col = jnp.arange(width)
    flip = ((col[:, None] + half) % width == col[None, :]).astype(rows.dtype)
    flip = flip * jnp.where(col[None, :] < half, -sign, sign).astype(rows.dtype)
    return jnp.einsum("...ki,kl->...li", rows, flip, preferred_element_type=jnp.float32).astype(rows.dtype)


def slot_ranks(target_peer, devices):
    count = target_peer.shape[-1]
    earlier = jnp.arange(count)[None, :] < jnp.arange(count)[:, None]
    same = target_peer[:, None] == target_peer[None, :]
    return jnp.sum((earlier & same).astype(jnp.int32), axis=1)


def with_header(blocks, values, devices, capacity):
    rows, lanes = blocks.shape[1], blocks.shape[2]
    body = blocks.reshape(devices, capacity * rows, lanes)
    head = jnp.pad(values.astype(blocks.dtype)[:, None, :], ((0, 0), (0, 15), (0, lanes - values.shape[1])))
    return jnp.concatenate([body, head], axis=1)


def split_header(buffer, capacity, rows, width):
    body = buffer[:, : capacity * rows].reshape(-1, rows, buffer.shape[2])
    return body, buffer[:, capacity * rows, :width]


def exchange(blocks, devices, direction):
    return jnp.stack(exchange_blocks(blocks, devices, direction))


def exchange_blocks(blocks, devices, direction):
    received = [blocks[0]]
    for shift in range(1, devices):
        pairs = [(i, (i + direction * shift) % devices) for i in range(devices)]
        received.append(lax.ppermute(blocks[shift], "spk", pairs))
    return received


def per_device(direction, plant, tile_pairs, mic_weight):
    devices = lax.axis_size("spk")
    device_id = lax.axis_index("spk")
    unit_count = direction.shape[0]
    tile_count = plant.shape[0]
    block_size = direction.shape[1]
    field_width = direction.shape[2]
    groups_per_bin = SBLK // unit_count
    bin_count = devices // groups_per_bin
    peer_blocks = MBLK // devices
    mic_units = bin_count * peer_blocks
    my_bin = device_id // groups_per_bin
    capacity = max(3, (2 * tile_count + devices - 1) // devices)
    slots = devices * capacity

    local_unit = tile_pairs[:, 0] % unit_count
    mic_block = tile_pairs[:, 1]
    target_peer = mic_block // peer_blocks
    shift_of = (target_peer - device_id) % devices
    position = shift_of * capacity + slot_ranks(target_peer, devices)
    send_hit = position[None, :] == jnp.arange(slots)[:, None]
    slot_pair = jnp.sum(jnp.where(send_hit, jnp.arange(tile_count), 0), axis=1)
    target_label = my_bin * peer_blocks + mic_block - target_peer * peer_blocks
    slot_label = jnp.where(
        send_hit.any(axis=1), jnp.sum(jnp.where(send_hit, target_label, 0), axis=1), mic_units
    )

    rounded = jnp.swapaxes(direction.astype(jnp.bfloat16), 1, 2)
    both = jnp.stack([rounded, swap_halves(rounded, 1)], axis=1)
    pair_rows = both[local_unit]
    partial_field = jnp.einsum("tcij,tckj->tki", plant, pair_rows,
                               preferred_element_type=jnp.float32).astype(jnp.bfloat16)
    outgoing = jnp.take(partial_field, slot_pair, axis=0, mode="clip")
    local_power = jnp.trace(jnp.einsum("tcij,tcik->jk", plant, plant,
                                       preferred_element_type=jnp.float32))
    power_hi = local_power.astype(jnp.bfloat16).astype(jnp.float32)
    power_mid = (local_power - power_hi).astype(jnp.bfloat16).astype(jnp.float32)
    power_lo = local_power - power_hi - power_mid
    power_parts = jnp.broadcast_to(jnp.stack([power_hi, power_mid, power_lo]), (devices, 3))
    header = jnp.concatenate([slot_label.reshape(devices, capacity).astype(jnp.float32), power_parts], axis=1)
    sent = with_header(outgoing, header, devices, capacity)
    arrived, header_in = split_header(exchange(sent, devices, 1), capacity, field_width, capacity + 3)
    labels_in = header_in[:, :capacity].astype(jnp.int32).reshape(slots)
    source_bin = ((device_id - jnp.arange(devices)) % devices) // groups_per_bin
    power_of = jnp.sum(header_in[:, capacity:].astype(jnp.float32), axis=1)
    bin_power = jnp.sum(jnp.where(source_bin == my_bin, power_of, 0.0))
    recv_onehot = (labels_in[None, :] == jnp.arange(mic_units)[:, None]).astype(jnp.bfloat16)
    pressure = jnp.einsum("ms,ski->mki", recv_onehot, arrived, preferred_element_type=jnp.float32)
    weights_flat = mic_weight.reshape(mic_units, block_size)
    weighted = (weights_flat[:, None, :] * pressure).astype(jnp.bfloat16)

    reply = jnp.take(weighted, jnp.minimum(labels_in, mic_units - 1), axis=0, mode="clip")
    returned = exchange_blocks(reply.reshape(devices, capacity * field_width, block_size), devices, -1)

    plant_by_slot = jnp.take(plant, slot_pair, axis=0, mode="clip")
    slot_unit = jnp.take(local_unit, slot_pair, axis=0, mode="clip")
    slot_mask = ((slot_unit[:, None] == jnp.arange(unit_count)[None, :])
                 & send_hit.any(axis=1)[:, None]).astype(jnp.bfloat16)
    gram = None
    for shift in range(devices):
        rows = returned[shift].reshape(capacity, field_width, block_size)
        back_rows = jnp.stack([rows, swap_halves(rows, -1)], axis=1)
        window = slice(shift * capacity, (shift + 1) * capacity)
        masked = back_rows[:, None] * slot_mask[window][:, :, None, None, None]
        part = jnp.einsum("scij,sucki->ujk", plant_by_slot[window], masked,
                          preferred_element_type=jnp.float32)
        gram = part if gram is None else gram + part
    return gram + reg_weight * bin_power / SPEAKERS * direction


def solution(mesh):
    placed = (
        P(("band", "spk"), None, None),
        P(("band", "spk"), None, None, None),
        P(("band", "spk"), None),
        P("band", "spk", None),
    )
    return jax.shard_map(
        per_device,
        mesh=mesh,
        in_specs=placed,
        out_specs=P(("band", "spk"), None, None),
        check_vma=False,
    )
```

```python
import jax
import jax.numpy as jnp
from jax import lax
from jax.sharding import PartitionSpec as P


SBLK = 32
MBLK = 128
SPEAKERS = 4096


reg_weight = 0.25


def swap_halves(rows, sign):
    width = rows.shape[-2]
    half = width // 2
    col = jnp.arange(width)
    flip = ((col[:, None] + half) % width == col[None, :]).astype(rows.dtype)
    flip = flip * jnp.where(col[None, :] < half, -sign, sign).astype(rows.dtype)
    return jnp.einsum("...ki,kl->...li", rows, flip, preferred_element_type=jnp.float32).astype(rows.dtype)


def slot_ranks(target_peer, devices):
    count = target_peer.shape[-1]
    earlier = jnp.arange(count)[None, :] < jnp.arange(count)[:, None]
    same = target_peer[:, None] == target_peer[None, :]
    return jnp.sum((earlier & same).astype(jnp.int32), axis=1)


def with_header(blocks, values, devices, capacity):
    rows, lanes = blocks.shape[1], blocks.shape[2]
    body = blocks.reshape(devices, capacity * rows, lanes)
    head = jnp.pad(values.astype(blocks.dtype)[:, None, :], ((0, 0), (0, 15), (0, lanes - values.shape[1])))
    return jnp.concatenate([body, head], axis=1)


def split_header(buffer, capacity, rows, width):
    body = buffer[:, : capacity * rows].reshape(-1, rows, buffer.shape[2])
    return body, buffer[:, capacity * rows, :width]


def exchange(blocks, devices, direction):
    received = [blocks[0]]
    for shift in range(1, devices):
        pairs = [(i, (i + direction * shift) % devices) for i in range(devices)]
        received.append(lax.ppermute(blocks[shift], "spk", pairs))
    return jnp.stack(received)


def per_device(direction, plant, tile_pairs, mic_weight):
    devices = lax.axis_size("spk")
    device_id = lax.axis_index("spk")
    unit_count = direction.shape[0]
    tile_count = plant.shape[0]
    block_size = direction.shape[1]
    field_width = direction.shape[2]
    groups_per_bin = SBLK // unit_count
    bin_count = devices // groups_per_bin
    peer_blocks = MBLK // devices
    mic_units = bin_count * peer_blocks
    my_bin = device_id // groups_per_bin
    capacity = max(3, (2 * tile_count + devices - 1) // devices)
    slots = devices * capacity

    local_unit = tile_pairs[:, 0] % unit_count
    mic_block = tile_pairs[:, 1]
    target_peer = mic_block // peer_blocks
    shift_of = (target_peer - device_id) % devices
    position = shift_of * capacity + slot_ranks(target_peer, devices)
    send_hit = position[None, :] == jnp.arange(slots)[:, None]
    slot_pair = jnp.sum(jnp.where(send_hit, jnp.arange(tile_count), 0), axis=1)
    target_label = my_bin * peer_blocks + mic_block - target_peer * peer_blocks
    slot_label = jnp.where(
        send_hit.any(axis=1), jnp.sum(jnp.where(send_hit, target_label, 0), axis=1), mic_units
    )

    rounded = jnp.swapaxes(direction.astype(jnp.bfloat16), 1, 2)
    both = jnp.stack([rounded, swap_halves(rounded, 1)], axis=1)
    pair_rows = both[local_unit]
    partial_field = jnp.einsum("tcij,tckj->tki", plant, pair_rows,
                               preferred_element_type=jnp.float32).astype(jnp.bfloat16)
    outgoing = jnp.take(partial_field, slot_pair, axis=0, mode="clip")
    plant_rows = plant.reshape(-1, block_size)
    local_power = jnp.trace(jnp.einsum("mj,mk->jk", plant_rows, plant_rows,
                                       preferred_element_type=jnp.float32))
    power_hi = local_power.astype(jnp.bfloat16).astype(jnp.float32)
    power_mid = (local_power - power_hi).astype(jnp.bfloat16).astype(jnp.float32)
    power_lo = local_power - power_hi - power_mid
    power_parts = jnp.broadcast_to(jnp.stack([power_hi, power_mid, power_lo]), (devices, 3))
    header = jnp.concatenate([slot_label.reshape(devices, capacity).astype(jnp.float32), power_parts], axis=1)
    sent = with_header(outgoing, header, devices, capacity)
    arrived, header_in = split_header(exchange(sent, devices, 1), capacity, field_width, capacity + 3)
    labels_in = header_in[:, :capacity].astype(jnp.int32).reshape(slots)
    source_bin = ((device_id - jnp.arange(devices)) % devices) // groups_per_bin
    power_of = jnp.sum(header_in[:, capacity:].astype(jnp.float32), axis=1)
    bin_power = jnp.sum(jnp.where(source_bin == my_bin, power_of, 0.0))
    recv_onehot = (labels_in[None, :] == jnp.arange(mic_units)[:, None]).astype(jnp.bfloat16)
    pressure = jnp.einsum("ms,ski->mki", recv_onehot, arrived, preferred_element_type=jnp.float32)
    weights_flat = mic_weight.reshape(mic_units, block_size)
    weighted = (weights_flat[:, None, :] * pressure).astype(jnp.bfloat16)

    reply = jnp.take(weighted, jnp.minimum(labels_in, mic_units - 1), axis=0, mode="clip")
    returned = exchange(reply.reshape(devices, capacity * field_width, block_size), devices, -1
                        ).reshape(slots, field_width, block_size)
    tile_weighted = jnp.take(returned, position, axis=0, mode="clip")

    back_rows = jnp.stack([tile_weighted, swap_halves(tile_weighted, -1)], axis=1)
    unit_mask = (local_unit[:, None] == jnp.arange(unit_count)[None, :]).astype(jnp.bfloat16)
    masked = back_rows[:, None] * unit_mask[:, :, None, None, None]
    gram = jnp.einsum("tcij,tucki->ujk", plant, masked, preferred_element_type=jnp.float32)
    return gram + reg_weight * bin_power / SPEAKERS * direction


def solution(mesh):
    placed = (
        P(("band", "spk"), None, None),
        P(("band", "spk"), None, None, None),
        P(("band", "spk"), None),
        P("band", "spk", None),
    )
    return jax.shard_map(
        per_device,
        mesh=mesh,
        in_specs=placed,
        out_specs=P(("band", "spk"), None, None),
        check_vma=False,
    )
```

```python
import jax
import jax.numpy as jnp
from jax import lax
from jax.sharding import PartitionSpec as P


SBLK = 32
MBLK = 128
SPEAKERS = 4096


reg_weight = 0.25


def swap_halves(rows, sign):
    width = rows.shape[-2]
    half = width // 2
    col = jnp.arange(width)
    flip = ((col[:, None] + half) % width == col[None, :]).astype(rows.dtype)
    flip = flip * jnp.where(col[None, :] < half, -sign, sign).astype(rows.dtype)
    return jnp.einsum("...ki,kl->...li", rows, flip, preferred_element_type=jnp.float32).astype(rows.dtype)


def slot_ranks(target_peer, devices):
    count = target_peer.shape[-1]
    earlier = jnp.arange(count)[None, :] < jnp.arange(count)[:, None]
    same = target_peer[:, None] == target_peer[None, :]
    return jnp.sum((earlier & same).astype(jnp.int32), axis=1)


def with_header(blocks, values, devices, capacity):
    rows, lanes = blocks.shape[1], blocks.shape[2]
    body = blocks.reshape(devices, capacity * rows, lanes)
    head = jnp.pad(values.astype(blocks.dtype)[:, None, :], ((0, 0), (0, 15), (0, lanes - values.shape[1])))
    return jnp.concatenate([body, head], axis=1)


def split_header(buffer, capacity, rows, width):
    body = buffer[:, : capacity * rows].reshape(-1, rows, buffer.shape[2])
    return body, buffer[:, capacity * rows, :width]


def exchange(blocks, devices, direction):
    received = [blocks[0]]
    for shift in range(1, devices):
        pairs = [(i, (i + direction * shift) % devices) for i in range(devices)]
        received.append(lax.ppermute(blocks[shift], "spk", pairs))
    return jnp.stack(received)


def per_device(direction, plant, tile_pairs, mic_weight):
    devices = lax.axis_size("spk")
    device_id = lax.axis_index("spk")
    unit_count = direction.shape[0]
    tile_count = plant.shape[0]
    block_size = direction.shape[1]
    field_width = direction.shape[2]
    groups_per_bin = SBLK // unit_count
    bin_count = devices // groups_per_bin
    peer_blocks = MBLK // devices
    mic_units = bin_count * peer_blocks
    my_bin = device_id // groups_per_bin
    capacity = max(3, (2 * tile_count + devices - 1) // devices)
    slots = devices * capacity

    local_unit = tile_pairs[:, 0] % unit_count
    mic_block = tile_pairs[:, 1]
    target_peer = mic_block // peer_blocks
    shift_of = (target_peer - device_id) % devices
    position = shift_of * capacity + slot_ranks(target_peer, devices)
    send_hit = position[None, :] == jnp.arange(slots)[:, None]
    slot_pair = jnp.sum(jnp.where(send_hit, jnp.arange(tile_count), 0), axis=1)
    target_label = my_bin * peer_blocks + mic_block - target_peer * peer_blocks
    slot_label = jnp.where(
        send_hit.any(axis=1), jnp.sum(jnp.where(send_hit, target_label, 0), axis=1), mic_units
    )

    rounded = jnp.swapaxes(direction.astype(jnp.bfloat16), 1, 2)
    both = jnp.stack([rounded, swap_halves(rounded, 1)], axis=1)
    pair_rows = both[local_unit]
    partial_field = jnp.einsum("tcij,tckj->tki", plant, pair_rows,
                               preferred_element_type=jnp.float32).astype(jnp.bfloat16)
    outgoing = jnp.take(partial_field, slot_pair, axis=0, mode="clip")
    local_power = jnp.sum(jnp.square(plant.astype(jnp.float32)))
    power_hi = local_power.astype(jnp.bfloat16).astype(jnp.float32)
    power_mid = (local_power - power_hi).astype(jnp.bfloat16).astype(jnp.float32)
    power_lo = local_power - power_hi - power_mid
    power_parts = jnp.broadcast_to(jnp.stack([power_hi, power_mid, power_lo]), (devices, 3))
    header = jnp.concatenate([slot_label.reshape(devices, capacity).astype(jnp.float32), power_parts], axis=1)
    sent = with_header(outgoing, header, devices, capacity)
    arrived, header_in = split_header(exchange(sent, devices, 1), capacity, field_width, capacity + 3)
    labels_in = header_in[:, :capacity].astype(jnp.int32).reshape(slots)
    source_bin = ((device_id - jnp.arange(devices)) % devices) // groups_per_bin
    power_of = jnp.sum(header_in[:, capacity:].astype(jnp.float32), axis=1)
    bin_power = jnp.sum(jnp.where(source_bin == my_bin, power_of, 0.0))
    recv_onehot = (labels_in[None, :] == jnp.arange(mic_units)[:, None]).astype(jnp.bfloat16)
    pressure = jnp.einsum("ms,ski->mki", recv_onehot, arrived, preferred_element_type=jnp.float32)
    weights_flat = mic_weight.reshape(mic_units, block_size)
    weighted = (weights_flat[:, None, :] * pressure).astype(jnp.bfloat16)

    reply = jnp.take(weighted, jnp.minimum(labels_in, mic_units - 1), axis=0, mode="clip")
    returned = exchange(reply.reshape(devices, capacity * field_width, block_size), devices, -1
                        ).reshape(slots, field_width, block_size)
    tile_weighted = jnp.take(returned, position, axis=0, mode="clip")

    back_rows = jnp.stack([tile_weighted, swap_halves(tile_weighted, -1)], axis=1)
    unit_mask = (local_unit[:, None] == jnp.arange(unit_count)[None, :]).astype(jnp.bfloat16)
    masked = back_rows[:, None] * unit_mask[:, :, None, None, None]
    gram = jnp.einsum("tcij,tucki->ujk", plant, masked, preferred_element_type=jnp.float32)
    return gram + reg_weight * bin_power / SPEAKERS * direction


def solution(mesh):
    placed = (
        P(("band", "spk"), None, None),
        P(("band", "spk"), None, None, None),
        P(("band", "spk"), None),
        P("band", "spk", None),
    )
    return jax.shard_map(
        per_device,
        mesh=mesh,
        in_specs=placed,
        out_specs=P(("band", "spk"), None, None),
        check_vma=False,
    )
```
